128 devices in a mesh: req: 16 (over z, x), mlp: 8 (over y, core).
Axes of the slice: x: 4, y: 4, z: 4, core: 2. Of those that a mesh axis runs over, the one named last changes fastest.
Arguments:
- residual_input: bfloat16 [9216, 5120], P('req', 'mlp'), as said below
- attention_output: bfloat16 [9216, 3072], P('req', 'mlp'), may hold values from -6 to 6
- request_length: int32 [16, 4], replicated, may hold values from 1 to 573, as said below
- request_group: int32 [64], replicated, may hold values from 0 to 7
- adapter_per_group: int32 [8], replicated, may hold values from 0 to 15
- output_weight: bfloat16 [3072, 5120], P('mlp', 'req'), may hold values from -0.109375 to 0.109375
- output_down_maps: bfloat16 [3072, 16, 16], P('mlp'), may hold values from -0.109375 to 0.109375
- output_up_maps: bfloat16 [16, 16, 5120], P(None, None, 'mlp'), may hold values from -1.5 to 1.5
- modulation: float32 [8, 3, 5120], replicated, may hold values from -3 to 3
- hidden_down_maps: bfloat16 [5120, 16, 16], P('mlp'), may hold values from -0.078125 to 0.078125
- hidden_up_maps: bfloat16 [16, 16, 6912], P(None, None, 'mlp'), may hold values from -1.5 to 1.5
- up_weight: bfloat16 [5120, 6912], P('req', 'mlp'), may hold values from -0.078125 to 0.078125
- down_weight: bfloat16 [6912, 5120], P('mlp', 'req'), may hold values from -0.078125 to 0.078125
Outputs:
- layer_out: bfloat16 [384, 16, 5120], P(None, 'req', 'mlp')
The draws below stay inside these ranges and needn't reach their ends.
Inputs may be any that keep to these rules, and one draw needn't show every extreme that they name: `request_length`: the 4 lengths of one block sum to at most 576, and to exactly 576 for one block; all lengths together sum to 6144. One request has exactly the largest length. `residual_input`: rows of a block past its live rows are never read.
All inputs are finite; a program needn't handle non-finite values.
Results may differ from the reference program's by a relative error of at most 0.012.
Values may be sent and summed in bfloat16 or wider, within the bound.
No kernel may reach another device: no remote copies, remote signals or barrier semaphores. Data moves between devices by JAX's collectives and lax.ppermute only.
A program may use at most 192 MiB of HBM per device.

```python
import jax
import jax.numpy as jnp
from jax import lax

MODEL_WIDTH = 5120
LOCAL_HEADS = 24
HEAD_WIDTH = 128
HIDDEN_SHARE = 6912
ADAPTER_RANK = 16
ADAPTER_TOTAL = 16
R_DEV = 4
TOK_DEV = 384
CAP = 576
TOKENS = 6144
GROUPS = 8
N_REQ = 16
N_MLP = 8


def draw_request_length(key, part):
    tok_block = TOK_DEV
    pair_count = N_REQ // 2
    keys = jax.random.split(jax.random.fold_in(key, 11), 5)
    spread = jax.random.randint(keys[0], (pair_count,), -(tok_block // 8), tok_block // 8 + 1)
    first = tok_block + spread
    second = tok_block - spread
    full_pair = jax.random.randint(keys[1], (), 0, pair_count)
    cut_pair = (full_pair + 1 + jax.random.randint(keys[2], (), 0, pair_count - 1)) % pair_count
    full_side = jax.random.randint(keys[3], (), 0, 2)
    pair_ids = jnp.arange(pair_count)
    is_full = pair_ids == full_pair
    is_cut = pair_ids == cut_pair
    big_value = 3 * tok_block // 2
    small_value = 3 * tok_block // 4
    first = jnp.where(is_full, jnp.where(full_side == 0, big_value, small_value), first)
    second = jnp.where(is_full, jnp.where(full_side == 0, small_value, big_value), second)
    first = jnp.where(is_cut, first - tok_block // 8, first)
    second = jnp.where(is_cut, second - tok_block // 8, second)
    live_rows = jnp.stack([first, second], axis=1).reshape(N_REQ)
    weights = jax.random.randint(keys[4], (N_REQ, R_DEV), 1, 4)
    weight_sum = jnp.sum(weights, axis=1, keepdims=True)
    pieces = live_rows[:, None] * weights // weight_sum
    remainder = live_rows - jnp.sum(pieces, axis=1)
    last_column = jnp.arange(R_DEV)[None, :] == R_DEV - 1
    pieces = pieces + jnp.where(last_column, remainder[:, None], 0)
    full_block = 2 * full_pair + full_side
    block_ids = jnp.arange(N_REQ)[:, None]
    column_ids = jnp.arange(R_DEV)[None, :]
    full_row = jnp.where(column_ids == 0, CAP - R_DEV + 1, 1)
    pieces = jnp.where(block_ids == full_block, full_row, pieces)
    return pieces.astype(jnp.int32)


def draw_residual_input(key, part):
    row_count = N_REQ * CAP
    keys = jax.random.split(jax.random.fold_in(key, 23), 3)
    base = jax.random.normal(keys[0], (row_count, MODEL_WIDTH), jnp.float32)
    row_scale = jnp.exp(jax.random.uniform(keys[1], (row_count, 1), jnp.float32, -1.15, 1.15))
    column_scale = jnp.exp(jax.random.uniform(keys[2], (1, MODEL_WIDTH), jnp.float32, -1.15, 1.15))
    return (base * row_scale * column_scale).astype(jnp.bfloat16)


def plant(drawn, stream_key, least, top_value):
    spot = [jax.random.randint(jax.random.fold_in(stream_key, axis), (), 0, length) for axis, length in enumerate(drawn.shape)]
    longest = drawn.shape.index(max(drawn.shape))
    neighbour = spot[:longest] + [(spot[longest] + 1) % drawn.shape[longest]] + spot[longest + 1:]
    return drawn.at[tuple(spot)].set(least).at[tuple(neighbour)].set(top_value)


def steps_of(rng, extent, cuts, smallest, top_value):
    gain = 1.0
    for dim, shards_of in cuts:
        draws = jax.random.uniform(jax.random.fold_in(jax.random.fold_in(rng, 6), dim), (shards_of,), jnp.float32, smallest / len(cuts), top_value / len(cuts))
        gain = gain * jnp.repeat(jnp.exp(draws), extent[dim] // shards_of).reshape((-1,) + (1,) * (len(extent) - 1 - dim))
    return gain


def gaussian(own_key, shape, deviation, bound, cuts=(), kind=jnp.bfloat16):
    array = jax.random.normal(own_key, shape, jnp.float32) * deviation
    if len(cuts) > 0:
        array = steps_of(own_key, shape, cuts, -0.22, 0.18) * array
    return jnp.clip(array, min=-bound, max=bound).astype(kind)


def setup_inputs(seed: int = 0) -> dict:
    seeds = jax.random.split(jax.random.key(seed), 14)
    return {
        "residual_input": draw_residual_input(jax.random.fold_in(seeds[13], 71), 0),
        "attention_output": gaussian(seeds[1], (N_REQ * CAP, LOCAL_HEADS * HEAD_WIDTH), 1.0, 6.0, ((0, 16), (1, 8))),
        "request_length": draw_request_length(jax.random.fold_in(seeds[13], 71), 0),
        "request_group": plant(jax.random.randint(seeds[3], (N_REQ * R_DEV,), 0, GROUPS), jax.random.fold_in(seeds[3], 1), 0, GROUPS - 1).astype(jnp.int32),
        "adapter_per_group": plant(jax.random.randint(seeds[4], (GROUPS,), 0, ADAPTER_TOTAL), jax.random.fold_in(seeds[4], 1), 0, ADAPTER_TOTAL - 1).astype(jnp.int32),
        "output_weight": gaussian(seeds[5], (LOCAL_HEADS * HEAD_WIDTH, MODEL_WIDTH), (LOCAL_HEADS * HEAD_WIDTH) ** -0.5, 0.109375, ((0, 8), (1, 16))),
        "output_down_maps": gaussian(seeds[6], (LOCAL_HEADS * HEAD_WIDTH, ADAPTER_TOTAL, ADAPTER_RANK), (LOCAL_HEADS * HEAD_WIDTH) ** -0.5, 0.109375, ((0, 8),)),
        "output_up_maps": gaussian(seeds[7], (ADAPTER_TOTAL, ADAPTER_RANK, MODEL_WIDTH), ADAPTER_RANK ** -0.5, 1.5, ((2, 8),)),
        "modulation": gaussian(seeds[8], (GROUPS, 3, MODEL_WIDTH), 0.5, 3.0, (), jnp.float32),
        "hidden_down_maps": gaussian(seeds[9], (MODEL_WIDTH, ADAPTER_TOTAL, ADAPTER_RANK), MODEL_WIDTH ** -0.5, 0.078125, ((0, 8),)),
        "hidden_up_maps": gaussian(seeds[10], (ADAPTER_TOTAL, ADAPTER_RANK, HIDDEN_SHARE), ADAPTER_RANK ** -0.5, 1.5, ((2, 8),)),
        "up_weight": gaussian(seeds[11], (MODEL_WIDTH, HIDDEN_SHARE), MODEL_WIDTH ** -0.5, 0.078125, ((0, 16), (1, 8))),
        "down_weight": gaussian(seeds[12], (HIDDEN_SHARE, MODEL_WIDTH), HIDDEN_SHARE ** -0.5, 0.078125, ((0, 8), (1, 16))),
    }


norm_epsilon = 1e-06

def round_keep(values):
    rounded = lax.optimization_barrier(values.astype(jnp.bfloat16))
    return rounded.astype(jnp.float32)

def expand_rank_rows(low_rows, adapter_of_row):
    adapter_hot = (adapter_of_row[:, None] == jnp.arange(ADAPTER_TOTAL, dtype=jnp.int32)[None, :]).astype(low_rows.dtype)
    return (adapter_hot[:, :, None] * low_rows[:, None, :]).reshape(low_rows.shape[0], ADAPTER_TOTAL * ADAPTER_RANK)

def select_low(output_rank_rows, adapter_of_row):
    adapter_hot = (adapter_of_row[:, None] == jnp.arange(ADAPTER_TOTAL, dtype=jnp.int32)[None, :]).astype(output_rank_rows.dtype)
    shaped = output_rank_rows.reshape(output_rank_rows.shape[0], ADAPTER_TOTAL, ADAPTER_RANK)
    return lax.optimization_barrier(jnp.sum(shaped * adapter_hot[:, :, None], axis=1))

def reference(residual_input, attention_output, request_length, request_group, adapter_per_group, output_weight, output_down_maps, output_up_maps, modulation, hidden_down_maps, hidden_up_maps, up_weight, down_weight):
    live_rows = lax.optimization_barrier(jnp.sum(request_length, axis=1))
    dev_ends = jnp.cumsum(live_rows)
    dev_starts = dev_ends - live_rows
    token_rank = jnp.arange(TOKENS, dtype=jnp.int32)
    owner = lax.optimization_barrier(jnp.sum((dev_ends[None, :] <= token_rank[:, None]).astype(jnp.int32), axis=1)).astype(jnp.int32)
    row_index = (owner * CAP + token_rank - dev_starts[owner]).astype(jnp.int32)
    attention_rows = attention_output[row_index]
    residual_rows = residual_input[row_index]
    req_ends = jnp.cumsum(request_length.reshape(-1))
    request = lax.optimization_barrier(jnp.sum((req_ends[None, :] <= token_rank[:, None]).astype(jnp.int32), axis=1))
    request = jnp.minimum(request, N_REQ * R_DEV - 1).astype(jnp.int32)
    group_ids = request_group[request]
    adapter_of_row = adapter_per_group[group_ids].astype(jnp.int32)
    mod_rows = modulation[group_ids]
    head_feature_width = LOCAL_HEADS * HEAD_WIDTH
    head_block = head_feature_width // N_MLP
    projection_rows = jnp.zeros((TOKENS, MODEL_WIDTH), jnp.float32)
    for block_index in range(N_MLP):
        lo_col = block_index * head_block
        term = jnp.dot(attention_rows[:, lo_col:lo_col + head_block], output_weight[lo_col:lo_col + head_block], preferred_element_type=jnp.float32)
        projection_rows = projection_rows + round_keep(term)
    output_rank_rows = jnp.dot(attention_rows, output_down_maps.reshape(head_feature_width, ADAPTER_TOTAL * ADAPTER_RANK), preferred_element_type=jnp.float32)
    output_rank_values = select_low(output_rank_rows, adapter_of_row).astype(jnp.bfloat16)
    adapter_delta = jnp.dot(expand_rank_rows(output_rank_values, adapter_of_row), output_up_maps.reshape(ADAPTER_TOTAL * ADAPTER_RANK, MODEL_WIDTH), preferred_element_type=jnp.float32)
    blended_rows = (residual_rows.astype(jnp.float32) + projection_rows + adapter_delta).astype(jnp.bfloat16)
    values = blended_rows.astype(jnp.float32)
    row_mean = lax.optimization_barrier(jnp.sum(values, axis=1, keepdims=True)) / MODEL_WIDTH
    variance = lax.optimization_barrier(jnp.sum(values * values, axis=1, keepdims=True)) / MODEL_WIDTH - row_mean * row_mean
    normalized_rows = ((values - row_mean) * lax.rsqrt(variance + norm_epsilon) * (1.0 + mod_rows[:, 1]) + mod_rows[:, 0]).astype(jnp.bfloat16)
    hidden_rank_rows = jnp.dot(normalized_rows, hidden_down_maps.reshape(MODEL_WIDTH, ADAPTER_TOTAL * ADAPTER_RANK), preferred_element_type=jnp.float32)
    hidden_rank_values = select_low(hidden_rank_rows, adapter_of_row).astype(jnp.bfloat16)
    hidden_total = jnp.dot(normalized_rows, up_weight, preferred_element_type=jnp.float32)
    hidden_total = hidden_total + jnp.dot(expand_rank_rows(hidden_rank_values, adapter_of_row), hidden_up_maps.reshape(ADAPTER_TOTAL * ADAPTER_RANK, HIDDEN_SHARE), preferred_element_type=jnp.float32)
    hidden = jax.nn.gelu(hidden_total, approximate=True).astype(jnp.bfloat16)
    hidden_block = HIDDEN_SHARE // N_MLP
    down_sum = jnp.zeros((TOKENS, MODEL_WIDTH), jnp.float32)
    for block_index in range(N_MLP):
        lo_col = block_index * hidden_block
        term = jnp.dot(hidden[:, lo_col:lo_col + hidden_block], down_weight[lo_col:lo_col + hidden_block], preferred_element_type=jnp.float32)
        down_sum = down_sum + round_keep(term)
    layer_out = (values + mod_rows[:, 2] * down_sum).astype(jnp.bfloat16)
    return layer_out.reshape(TOK_DEV, N_REQ, MODEL_WIDTH)
```

```python
import jax
import jax.numpy as jnp
from jax import lax
from jax.sharding import PartitionSpec as P

MODEL_WIDTH = 5120
ADAPTER_RANK = 16
ADAPTER_TOTAL = 16
TOK_DEV = 384


norm_epsilon = 1e-06


def send_layout(packed, offset, req_count):
    shaped = packed.reshape(packed.shape[0] // req_count, req_count, packed.shape[1])
    return jnp.roll(shaped, offset, axis=1)


def compact(moved, starts, ends, req_count, token_rank):
    slots = moved.shape[0] * moved.shape[1]
    flat_rows = moved.reshape(slots, moved.shape[2])
    source = jnp.sum((ends[None, :] <= token_rank[:, None]).astype(jnp.int32), axis=1)
    source_hot = source[:, None] == jnp.arange(req_count, dtype=jnp.int32)[None, :]
    source_start = jnp.sum(jnp.where(source_hot, starts[None, :], 0), axis=1)
    position = (token_rank - source_start) // req_count * req_count + source
    return jnp.take(flat_rows, position, axis=0)


def token_groups(token_rank, request_length, request_group, adapter_per_group):
    req_ends = jnp.cumsum(request_length.reshape(-1))
    request_count = req_ends.shape[0]
    request = jnp.sum((req_ends[None, :] <= token_rank[:, None]).astype(jnp.int32), axis=1)
    request = jnp.minimum(request, request_count - 1)
    request_hot = request[:, None] == jnp.arange(request_count, dtype=jnp.int32)[None, :]
    group_ids = jnp.sum(jnp.where(request_hot, request_group[None, :], 0), axis=1)
    group_count = adapter_per_group.shape[0]
    group_hot = group_ids[:, None] == jnp.arange(group_count, dtype=jnp.int32)[None, :]
    adapter_of_row = jnp.sum(jnp.where(group_hot, adapter_per_group[None, :], 0), axis=1)
    adapter_hot = (
        adapter_of_row[:, None] == jnp.arange(ADAPTER_TOTAL, dtype=jnp.int32)[None, :]
    ).astype(jnp.float32)
    return group_ids, adapter_hot


def select_low(output_rank_rows, adapter_hot):
    shaped = output_rank_rows.reshape(output_rank_rows.shape[0], ADAPTER_TOTAL, ADAPTER_RANK)
    return jnp.sum(shaped * adapter_hot[:, :, None], axis=1)


def expand_rank_rows(low_rows, adapter_hot):
    spread_rows = adapter_hot.astype(jnp.bfloat16)[:, :, None] * low_rows[:, None, :]
    return spread_rows.reshape(low_rows.shape[0], ADAPTER_TOTAL * ADAPTER_RANK)


def mlp_sum(part):
    n = lax.axis_size("mlp")
    total = part.astype(jnp.float32)
    for k in range(1, n):
        moved = lax.ppermute(part, "mlp", [(i, (i + k) % n) for i in range(n)])
        total = total + moved.astype(jnp.float32)
    return total


def local(
    residual_input,
    attention_output,
    request_length,
    request_group,
    adapter_per_group,
    output_weight,
    output_down_maps,
    output_up_maps,
    modulation,
    hidden_down_maps,
    hidden_up_maps,
    up_weight,
    down_weight,
):
    req_count = lax.axis_size("req")
    mlp_count = lax.axis_size("mlp")
    device_index = lax.axis_index("req")
    column_index = lax.axis_index("mlp")
    width = residual_input.shape[1]
    head_width = attention_output.shape[1]

    out_w = lax.all_gather(output_weight, "req", axis=1, tiled=True)
    up_w = lax.all_gather(up_weight, "req", axis=0, tiled=True)
    down_w = lax.all_gather(down_weight, "req", axis=1, tiled=True)

    live_rows = jnp.sum(request_length, axis=1)
    dev_ends = jnp.cumsum(live_rows)
    dev_starts = dev_ends - live_rows
    offset = dev_starts[device_index]
    tok_dev = TOK_DEV
    token_rank = jnp.arange(tok_dev, dtype=jnp.int32) * req_count + device_index
    moved_attn = lax.all_to_all(
        send_layout(attention_output, offset, req_count), "req", split_axis=1, concat_axis=1, tiled=True
    )
    attention_rows = compact(moved_attn, dev_starts, dev_ends, req_count, token_rank)
    moved_res = lax.all_to_all(
        send_layout(residual_input, offset, req_count), "req", split_axis=1, concat_axis=1, tiled=True
    )
    residual_rows = compact(moved_res, dev_starts, dev_ends, req_count, token_rank)

    group_ids, adapter_hot = token_groups(token_rank, request_length, request_group, adapter_per_group)
    shift_rows = jnp.take(modulation[:, 0, :], group_ids, axis=0)
    scale_rows = jnp.take(modulation[:, 1, :], group_ids, axis=0)
    gate_table = lax.dynamic_slice_in_dim(modulation[:, 2, :], column_index * width, width, 1)
    gate_rows = jnp.take(gate_table, group_ids, axis=0)

    head_terms = jnp.einsum(
        "tk,kmc->mtc",
        attention_rows,
        out_w.reshape(head_width, mlp_count, width),
        preferred_element_type=jnp.float32,
    )
    out_low = select_low(
        jnp.dot(
            attention_rows,
            output_down_maps.reshape(head_width, ADAPTER_TOTAL * ADAPTER_RANK),
            preferred_element_type=jnp.float32,
        ),
        adapter_hot,
    )
    send = jnp.concatenate(
        [head_terms, jnp.broadcast_to(out_low[None], (mlp_count,) + out_low.shape)], axis=2
    ).astype(jnp.bfloat16)
    summed = lax.psum_scatter(send, "mlp", scatter_dimension=0, tiled=True)[0]
    projection_rows = summed[:, :width].astype(jnp.float32)
    output_rank_values = summed[:, width:]
    adapter_delta = jnp.dot(
        expand_rank_rows(output_rank_values, adapter_hot),
        output_up_maps.reshape(ADAPTER_TOTAL * ADAPTER_RANK, width),
        preferred_element_type=jnp.float32,
    )
    blended_rows = (residual_rows.astype(jnp.float32) + projection_rows + adapter_delta).astype(
        jnp.bfloat16
    )
    values = blended_rows.astype(jnp.float32)

    full_rows = lax.all_gather(blended_rows, "mlp", axis=0, tiled=False).astype(jnp.float32)
    row_mean = jnp.sum(full_rows, axis=(0, 2)) / MODEL_WIDTH
    variance = jnp.sum(full_rows * full_rows, axis=(0, 2)) / MODEL_WIDTH - row_mean * row_mean
    inv = lax.rsqrt(variance + norm_epsilon)
    scale_m = (1.0 + scale_rows).reshape(-1, mlp_count, width).transpose(1, 0, 2)
    shift_m = shift_rows.reshape(-1, mlp_count, width).transpose(1, 0, 2)
    normalized = (
        (full_rows - row_mean[None, :, None]) * inv[None, :, None] * scale_m + shift_m
    ).astype(jnp.bfloat16)

    normed_local = lax.dynamic_index_in_dim(normalized, column_index, 0, keepdims=False)
    part_low = jnp.dot(
        normed_local,
        hidden_down_maps.reshape(width, ADAPTER_TOTAL * ADAPTER_RANK),
        preferred_element_type=jnp.float32,
    )
    hidden_rank_values = mlp_sum(select_low(part_low, adapter_hot).astype(jnp.bfloat16)).astype(
        jnp.bfloat16
    )
    hidden_units = up_weight.shape[1]
    hidden_total = jnp.einsum(
        "mtc,mch->th",
        normalized,
        up_w.reshape(mlp_count, width, hidden_units),
        preferred_element_type=jnp.float32,
    )
    hidden_total = hidden_total + jnp.dot(
        expand_rank_rows(hidden_rank_values, adapter_hot),
        hidden_up_maps.reshape(ADAPTER_TOTAL * ADAPTER_RANK, hidden_units),
        preferred_element_type=jnp.float32,
    )
    hidden = jax.nn.gelu(hidden_total, approximate=True).astype(jnp.bfloat16)
    down_terms = jnp.einsum(
        "th,hmc->mtc",
        hidden,
        down_w.reshape(hidden_units, mlp_count, width),
        preferred_element_type=jnp.float32,
    ).astype(jnp.bfloat16)
    down_sum = lax.psum_scatter(down_terms, "mlp", scatter_dimension=0, tiled=True)[0].astype(
        jnp.float32
    )
    result = (values + gate_rows * down_sum).astype(jnp.bfloat16)
    return result.reshape(tok_dev, 1, width)


def solution(mesh):
    placed = (
        P("req", "mlp"),
        P("req", "mlp"),
        P(),
        P(),
        P(),
        P("mlp", "req"),
        P("mlp", None, None),
        P(None, None, "mlp"),
        P(),
        P("mlp", None, None),
        P(None, None, "mlp"),
        P("req", "mlp"),
        P("mlp", "req"),
    )
    return jax.shard_map(
        local, mesh=mesh, in_specs=placed, out_specs=P(None, "req", "mlp"), check_vma=False
    )
```

```python
import jax
import jax.numpy as jnp
from jax import lax
from jax.sharding import PartitionSpec as P

MODEL_WIDTH = 5120
ADAPTER_RANK = 16
ADAPTER_TOTAL = 16
TOK_DEV = 384
Z_COUNT = 4


norm_epsilon = 1e-06


def send_layout(packed, offset, req_count):
    shaped = packed.reshape(packed.shape[0] // req_count, req_count, packed.shape[1])
    return jnp.roll(shaped, offset, axis=1)


def compact(moved, starts, ends, req_count, token_rank):
    slots = moved.shape[0] * moved.shape[1]
    flat_rows = moved.reshape(slots, moved.shape[2])
    source = jnp.sum((ends[None, :] <= token_rank[:, None]).astype(jnp.int32), axis=1)
    source_hot = source[:, None] == jnp.arange(req_count, dtype=jnp.int32)[None, :]
    source_start = jnp.sum(jnp.where(source_hot, starts[None, :], 0), axis=1)
    position = (token_rank - source_start) // req_count * req_count + source
    return jnp.take(flat_rows, position, axis=0)


def token_groups(token_rank, request_length, request_group, adapter_per_group):
    req_ends = jnp.cumsum(request_length.reshape(-1))
    request_count = req_ends.shape[0]
    request = jnp.sum((req_ends[None, :] <= token_rank[:, None]).astype(jnp.int32), axis=1)
    request = jnp.minimum(request, request_count - 1)
    request_hot = request[:, None] == jnp.arange(request_count, dtype=jnp.int32)[None, :]
    group_ids = jnp.sum(jnp.where(request_hot, request_group[None, :], 0), axis=1)
    group_count = adapter_per_group.shape[0]
    group_hot = group_ids[:, None] == jnp.arange(group_count, dtype=jnp.int32)[None, :]
    adapter_of_row = jnp.sum(jnp.where(group_hot, adapter_per_group[None, :], 0), axis=1)
    adapter_hot = (
        adapter_of_row[:, None] == jnp.arange(ADAPTER_TOTAL, dtype=jnp.int32)[None, :]
    ).astype(jnp.float32)
    return group_ids, adapter_hot


def select_low(output_rank_rows, adapter_hot):
    shaped = output_rank_rows.reshape(output_rank_rows.shape[0], ADAPTER_TOTAL, ADAPTER_RANK)
    return jnp.sum(shaped * adapter_hot[:, :, None], axis=1)


def expand_rank_rows(low_rows, adapter_hot):
    spread_rows = adapter_hot.astype(jnp.bfloat16)[:, :, None] * low_rows[:, None, :]
    return spread_rows.reshape(low_rows.shape[0], ADAPTER_TOTAL * ADAPTER_RANK)


def mlp_sum(part):
    n = lax.axis_size("mlp")
    total = part.astype(jnp.float32)
    for k in range(1, n):
        moved = lax.ppermute(part, "mlp", [(i, (i + k) % n) for i in range(n)])
        total = total + moved.astype(jnp.float32)
    return total


def shift(block, axis_sizes, along, step):
    z_count, x_count = axis_sizes
    pairs = []
    for z in range(z_count):
        for x in range(x_count):
            if along == "x":
                pairs.append((z * x_count + x, z * x_count + (x + step) % x_count))
            else:
                pairs.append((z * x_count + x, ((z + step) % z_count) * x_count + x))
    return lax.ppermute(block, "req", pairs)


def ring_row(stack, axis_sizes, along):
    from_left = shift(stack, axis_sizes, along, 1)
    from_right = shift(stack, axis_sizes, along, -1)
    n = stack.shape[0]
    if n >= 2:
        far_a = shift(from_left[: n // 2], axis_sizes, along, 1)
        far_b = shift(from_right[n // 2 :], axis_sizes, along, -1)
        far = jnp.concatenate([far_a, far_b], axis=0)
    else:
        cut = stack.shape[-1] // 2
        far_a = shift(from_left[..., :cut], axis_sizes, along, 1)
        far_b = shift(from_right[..., cut:], axis_sizes, along, -1)
        far = jnp.concatenate([far_a, far_b], axis=-1)
    return jnp.stack([stack, from_right, far, from_left], axis=0)


def gather_req(block, z_count, x_count):
    axis_sizes = (z_count, x_count)
    rows = block.shape[0]
    half_a = block[: rows // 2][None]
    half_b = block[rows // 2 :][None]
    row_a = ring_row(half_a, axis_sizes, "x")[:, 0]
    all_a = ring_row(row_a, axis_sizes, "z")
    row_b = ring_row(half_b, axis_sizes, "z")[:, 0]
    all_b = ring_row(row_b, axis_sizes, "x").transpose(1, 0, *range(2, block.ndim + 2))
    both = jnp.concatenate([all_a, all_b], axis=2)
    both = both.reshape((z_count * x_count,) + block.shape)
    r = lax.axis_index("req")
    z_here = r // x_count
    x_here = r % x_count
    target = jnp.arange(z_count * x_count, dtype=jnp.int32)
    rel = ((target // x_count - z_here) % z_count) * x_count + (target % x_count - x_here) % x_count
    return jnp.take(both, rel, axis=0)


def local(
    residual_input,
    attention_output,
    request_length,
    request_group,
    adapter_per_group,
    output_weight,
    output_down_maps,
    output_up_maps,
    modulation,
    hidden_down_maps,
    hidden_up_maps,
    up_weight,
    down_weight,
):
    req_count = lax.axis_size("req")
    mlp_count = lax.axis_size("mlp")
    device_index = lax.axis_index("req")
    column_index = lax.axis_index("mlp")
    width = residual_input.shape[1]
    head_width = attention_output.shape[1]

    out_w = gather_req(output_weight, Z_COUNT, req_count // Z_COUNT)
    up_w = gather_req(up_weight, Z_COUNT, req_count // Z_COUNT)
    down_w = gather_req(down_weight, Z_COUNT, req_count // Z_COUNT)

    live_rows = jnp.sum(request_length, axis=1)
    dev_ends = jnp.cumsum(live_rows)
    dev_starts = dev_ends - live_rows
    offset = dev_starts[device_index]
    tok_dev = TOK_DEV
    token_rank = jnp.arange(tok_dev, dtype=jnp.int32) * req_count + device_index
    moved_attn = lax.all_to_all(
        send_layout(attention_output, offset, req_count), "req", split_axis=1, concat_axis=1, tiled=True
    )
    attention_rows = compact(moved_attn, dev_starts, dev_ends, req_count, token_rank)
    moved_res = lax.all_to_all(
        send_layout(residual_input, offset, req_count), "req", split_axis=1, concat_axis=1, tiled=True
    )
    residual_rows = compact(moved_res, dev_starts, dev_ends, req_count, token_rank)

    group_ids, adapter_hot = token_groups(token_rank, request_length, request_group, adapter_per_group)
    shift_rows = jnp.take(modulation[:, 0, :], group_ids, axis=0)
    scale_rows = jnp.take(modulation[:, 1, :], group_ids, axis=0)
    gate_table = lax.dynamic_slice_in_dim(modulation[:, 2, :], column_index * width, width, 1)
    gate_rows = jnp.take(gate_table, group_ids, axis=0)

    piece = out_w.shape[2]
    head_terms = jnp.einsum(
        "tk,rkc->rtc", attention_rows, out_w, preferred_element_type=jnp.float32
    ).reshape(mlp_count, width // piece * tok_dev, piece)
    out_low = select_low(
        jnp.dot(
            attention_rows,
            output_down_maps.reshape(head_width, ADAPTER_TOTAL * ADAPTER_RANK),
            preferred_element_type=jnp.float32,
        ),
        adapter_hot,
    )
    low_count = out_low.size
    low_rows = -(-low_count // piece)
    low_flat = jnp.pad(out_low.reshape(-1), (0, low_rows * piece - low_count)).reshape(
        1, low_rows, piece
    )
    send = jnp.concatenate(
        [head_terms, jnp.broadcast_to(low_flat, (mlp_count, low_rows, piece))], axis=1
    ).astype(jnp.bfloat16)
    summed = lax.psum_scatter(send, "mlp", scatter_dimension=0, tiled=True)[0]
    projection_rows = (
        summed[: head_terms.shape[1]]
        .reshape(width // piece, tok_dev, piece)
        .transpose(1, 0, 2)
        .reshape(tok_dev, width)
        .astype(jnp.float32)
    )
    output_rank_values = summed[head_terms.shape[1] :].reshape(-1)[:low_count].reshape(
        tok_dev, ADAPTER_RANK
    )
    adapter_delta = jnp.dot(
        expand_rank_rows(output_rank_values, adapter_hot),
        output_up_maps.reshape(ADAPTER_TOTAL * ADAPTER_RANK, width),
        preferred_element_type=jnp.float32,
    )
    blended_rows = (residual_rows.astype(jnp.float32) + projection_rows + adapter_delta).astype(
        jnp.bfloat16
    )
    values = blended_rows.astype(jnp.float32)

    full_rows = lax.all_gather(blended_rows, "mlp", axis=0, tiled=False).astype(jnp.float32)
    row_mean = jnp.sum(full_rows, axis=(0, 2)) / MODEL_WIDTH
    variance = jnp.sum(full_rows * full_rows, axis=(0, 2)) / MODEL_WIDTH - row_mean * row_mean
    inv = lax.rsqrt(variance + norm_epsilon)
    scale_m = (1.0 + scale_rows).reshape(-1, mlp_count, width).transpose(1, 0, 2)
    shift_m = shift_rows.reshape(-1, mlp_count, width).transpose(1, 0, 2)
    normalized = (
        (full_rows - row_mean[None, :, None]) * inv[None, :, None] * scale_m + shift_m
    ).astype(jnp.bfloat16)

    normed_local = lax.dynamic_index_in_dim(normalized, column_index, 0, keepdims=False)
    part_low = jnp.dot(
        normed_local,
        hidden_down_maps.reshape(width, ADAPTER_TOTAL * ADAPTER_RANK),
        preferred_element_type=jnp.float32,
    )
    hidden_rank_values = mlp_sum(select_low(part_low, adapter_hot).astype(jnp.bfloat16)).astype(
        jnp.bfloat16
    )
    hidden_units = up_weight.shape[1]
    hidden_total = jnp.einsum(
        "mtc,mch->th",
        normalized,
        up_w.reshape(mlp_count, width, hidden_units),
        preferred_element_type=jnp.float32,
    )
    hidden_total = hidden_total + jnp.dot(
        expand_rank_rows(hidden_rank_values, adapter_hot),
        hidden_up_maps.reshape(ADAPTER_TOTAL * ADAPTER_RANK, hidden_units),
        preferred_element_type=jnp.float32,
    )
    hidden = jax.nn.gelu(hidden_total, approximate=True).astype(jnp.bfloat16)
    down_terms = jnp.einsum(
        "th,rhc->rtc", hidden, down_w, preferred_element_type=jnp.float32
    ).astype(jnp.bfloat16)
    piece = down_w.shape[2]
    down_terms = down_terms.reshape(mlp_count, width // piece, tok_dev, piece)
    down_sum = (
        lax.psum_scatter(down_terms, "mlp", scatter_dimension=0, tiled=True)[0]
        .transpose(1, 0, 2)
        .reshape(tok_dev, width)
        .astype(jnp.float32)
    )
    result = (values + gate_rows * down_sum).astype(jnp.bfloat16)
    return result.reshape(tok_dev, 1, width)


def solution(mesh):
    placed = (
        P("req", "mlp"),
        P("req", "mlp"),
        P(),
        P(),
        P(),
        P("mlp", "req"),
        P("mlp", None, None),
        P(None, None, "mlp"),
        P(),
        P("mlp", None, None),
        P(None, None, "mlp"),
        P("req", "mlp"),
        P("mlp", "req"),
    )
    return jax.shard_map(
        local, mesh=mesh, in_specs=placed, out_specs=P(None, "req", "mlp"), check_vma=False
    )
```

```python
import jax
import jax.numpy as jnp
from jax import lax
from jax.sharding import PartitionSpec as P

MODEL_WIDTH = 5120
ADAPTER_RANK = 16
ADAPTER_TOTAL = 16
TOK_DEV = 384
Z_COUNT = 4


norm_epsilon = 1e-06


def send_layout(packed, offset, req_count):
    shaped = packed.reshape(packed.shape[0] // req_count, req_count, packed.shape[1])
    return jnp.roll(shaped, offset, axis=1)


def compact(moved, starts, ends, req_count, token_rank):
    slots = moved.shape[0] * moved.shape[1]
    flat_rows = moved.reshape(slots, moved.shape[2])
    source = jnp.sum((ends[None, :] <= token_rank[:, None]).astype(jnp.int32), axis=1)
    source_hot = source[:, None] == jnp.arange(req_count, dtype=jnp.int32)[None, :]
    source_start = jnp.sum(jnp.where(source_hot, starts[None, :], 0), axis=1)
    position = (token_rank - source_start) // req_count * req_count + source
    return jnp.take(flat_rows, position, axis=0)


def token_groups(token_rank, request_length, request_group, adapter_per_group):
    req_ends = jnp.cumsum(request_length.reshape(-1))
    request_count = req_ends.shape[0]
    request = jnp.sum((req_ends[None, :] <= token_rank[:, None]).astype(jnp.int32), axis=1)
    request = jnp.minimum(request, request_count - 1)
    request_hot = request[:, None] == jnp.arange(request_count, dtype=jnp.int32)[None, :]
    group_ids = jnp.sum(jnp.where(request_hot, request_group[None, :], 0), axis=1)
    group_count = adapter_per_group.shape[0]
    group_hot = group_ids[:, None] == jnp.arange(group_count, dtype=jnp.int32)[None, :]
    adapter_of_row = jnp.sum(jnp.where(group_hot, adapter_per_group[None, :], 0), axis=1)
    adapter_hot = (
        adapter_of_row[:, None] == jnp.arange(ADAPTER_TOTAL, dtype=jnp.int32)[None, :]
    ).astype(jnp.float32)
    return group_ids, adapter_hot


def select_low(output_rank_rows, adapter_hot):
    shaped = output_rank_rows.reshape(output_rank_rows.shape[0], ADAPTER_TOTAL, ADAPTER_RANK)
    return jnp.sum(shaped * adapter_hot[:, :, None], axis=1)


def expand_rank_rows(low_rows, adapter_hot):
    spread_rows = adapter_hot.astype(jnp.bfloat16)[:, :, None] * low_rows[:, None, :]
    return spread_rows.reshape(low_rows.shape[0], ADAPTER_TOTAL * ADAPTER_RANK)


def mlp_sum(part):
    n = lax.axis_size("mlp")
    total = part.astype(jnp.float32)
    bit = 1
    while bit < n:
        total = total + lax.ppermute(total, "mlp", [(i, i ^ bit) for i in range(n)])
        bit *= 2
    return total


def shift(block, axis_sizes, along, step):
    z_count, x_count = axis_sizes
    pairs = []
    for z in range(z_count):
        for x in range(x_count):
            if along == "x":
                pairs.append((z * x_count + x, z * x_count + (x + step) % x_count))
            else:
                pairs.append((z * x_count + x, ((z + step) % z_count) * x_count + x))
    return lax.ppermute(block, "req", pairs)


def ring_row(stack, axis_sizes, along):
    from_left = shift(stack, axis_sizes, along, 1)
    from_right = shift(stack, axis_sizes, along, -1)
    n = stack.shape[0]
    if n >= 2:
        far_a = shift(from_left[: n // 2], axis_sizes, along, 1)
        far_b = shift(from_right[n // 2 :], axis_sizes, along, -1)
        far = jnp.concatenate([far_a, far_b], axis=0)
    else:
        cut = stack.shape[1] // 2
        far_a = shift(from_left[:, :cut], axis_sizes, along, 1)
        far_b = shift(from_right[:, cut:], axis_sizes, along, -1)
        far = jnp.concatenate([far_a, far_b], axis=1)
    return jnp.stack([stack, from_right, far, from_left], axis=0)


def gather_req(block, z_count, x_count, first):
    axis_sizes = (z_count, x_count)
    second = "z" if first == "x" else "x"
    row = ring_row(block[None], axis_sizes, first)[:, 0]
    both = ring_row(row, axis_sizes, second)
    both = both.reshape((z_count * x_count,) + block.shape)
    r = lax.axis_index("req")
    z_here = r // x_count
    x_here = r % x_count
    target = jnp.arange(z_count * x_count, dtype=jnp.int32)
    rel_z = (target // x_count - z_here) % z_count
    rel_x = (target % x_count - x_here) % x_count
    rel = rel_z * x_count + rel_x if first == "x" else rel_x * z_count + rel_z
    return jnp.take(both, rel, axis=0)


def local(
    residual_input,
    attention_output,
    request_length,
    request_group,
    adapter_per_group,
    output_weight,
    output_down_maps,
    output_up_maps,
    modulation,
    hidden_down_maps,
    hidden_up_maps,
    up_weight,
    down_weight,
):
    req_count = lax.axis_size("req")
    mlp_count = lax.axis_size("mlp")
    device_index = lax.axis_index("req")
    column_index = lax.axis_index("mlp")
    width = residual_input.shape[1]
    head_width = attention_output.shape[1]

    out_w = lax.all_gather(output_weight, "req", axis=0, tiled=False)
    up_w = gather_req(up_weight, Z_COUNT, req_count // Z_COUNT, "x")
    down_w = gather_req(down_weight, Z_COUNT, req_count // Z_COUNT, "z")

    live_rows = jnp.sum(request_length, axis=1)
    dev_ends = jnp.cumsum(live_rows)
    dev_starts = dev_ends - live_rows
    offset = dev_starts[device_index]
    tok_dev = TOK_DEV
    token_rank = jnp.arange(tok_dev, dtype=jnp.int32) * req_count + device_index
    moved_attn = lax.all_to_all(
        send_layout(attention_output, offset, req_count), "req", split_axis=1, concat_axis=1, tiled=True
    )
    attention_rows = compact(moved_attn, dev_starts, dev_ends, req_count, token_rank)
    moved_res = lax.all_to_all(
        send_layout(residual_input, offset, req_count), "req", split_axis=1, concat_axis=1, tiled=True
    )
    residual_rows = compact(moved_res, dev_starts, dev_ends, req_count, token_rank)

    group_ids, adapter_hot = token_groups(token_rank, request_length, request_group, adapter_per_group)
    shift_rows = jnp.take(modulation[:, 0, :], group_ids, axis=0)
    scale_rows = jnp.take(modulation[:, 1, :], group_ids, axis=0)
    gate_table = lax.dynamic_slice_in_dim(modulation[:, 2, :], column_index * width, width, 1)
    gate_rows = jnp.take(gate_table, group_ids, axis=0)

    piece = out_w.shape[2]
    head_terms = jnp.einsum(
        "tk,rkc->rtc", attention_rows, out_w, preferred_element_type=jnp.float32
    ).reshape(mlp_count, width // piece * tok_dev, piece)
    out_low = select_low(
        jnp.dot(
            attention_rows,
            output_down_maps.reshape(head_width, ADAPTER_TOTAL * ADAPTER_RANK),
            preferred_element_type=jnp.float32,
        ),
        adapter_hot,
    )
    low_count = out_low.size
    low_rows = -(-low_count // piece)
    low_flat = jnp.pad(out_low.reshape(-1), (0, low_rows * piece - low_count)).reshape(
        1, low_rows, piece
    )
    send = jnp.concatenate(
        [head_terms, jnp.broadcast_to(low_flat, (mlp_count, low_rows, piece))], axis=1
    ).astype(jnp.bfloat16)
    summed = lax.psum_scatter(send, "mlp", scatter_dimension=0, tiled=True)[0]
    projection_rows = (
        summed[: head_terms.shape[1]]
        .reshape(width // piece, tok_dev, piece)
        .transpose(1, 0, 2)
        .reshape(tok_dev, width)
        .astype(jnp.float32)
    )
    output_rank_values = summed[head_terms.shape[1] :].reshape(-1)[:low_count].reshape(
        tok_dev, ADAPTER_RANK
    )
    adapter_delta = jnp.dot(
        expand_rank_rows(output_rank_values, adapter_hot),
        output_up_maps.reshape(ADAPTER_TOTAL * ADAPTER_RANK, width),
        preferred_element_type=jnp.float32,
    )
    blended_rows = (residual_rows.astype(jnp.float32) + projection_rows + adapter_delta).astype(
        jnp.bfloat16
    )
    values = blended_rows.astype(jnp.float32)

    full_rows = lax.all_gather(blended_rows, "mlp", axis=0, tiled=False).astype(jnp.float32)
    row_mean = jnp.sum(full_rows, axis=(0, 2)) / MODEL_WIDTH
    variance = jnp.sum(full_rows * full_rows, axis=(0, 2)) / MODEL_WIDTH - row_mean * row_mean
    inv = lax.rsqrt(variance + norm_epsilon)
    scale_m = (1.0 + scale_rows).reshape(-1, mlp_count, width).transpose(1, 0, 2)
    shift_m = shift_rows.reshape(-1, mlp_count, width).transpose(1, 0, 2)
    normalized = (
        (full_rows - row_mean[None, :, None]) * inv[None, :, None] * scale_m + shift_m
    ).astype(jnp.bfloat16)

    normed_local = lax.dynamic_index_in_dim(normalized, column_index, 0, keepdims=False)
    part_low = jnp.dot(
        normed_local,
        hidden_down_maps.reshape(width, ADAPTER_TOTAL * ADAPTER_RANK),
        preferred_element_type=jnp.float32,
    )
    hidden_rank_values = mlp_sum(select_low(part_low, adapter_hot).astype(jnp.bfloat16)).astype(
        jnp.bfloat16
    )
    hidden_units = up_weight.shape[1]
    hidden_total = jnp.einsum(
        "mtc,mch->th",
        normalized,
        up_w.reshape(mlp_count, width, hidden_units),
        preferred_element_type=jnp.float32,
    )
    hidden_total = hidden_total + jnp.dot(
        expand_rank_rows(hidden_rank_values, adapter_hot),
        hidden_up_maps.reshape(ADAPTER_TOTAL * ADAPTER_RANK, hidden_units),
        preferred_element_type=jnp.float32,
    )
    hidden = jax.nn.gelu(hidden_total, approximate=True).astype(jnp.bfloat16)
    down_terms = jnp.einsum(
        "th,rhc->rtc", hidden, down_w, preferred_element_type=jnp.float32
    ).astype(jnp.bfloat16)
    piece = down_w.shape[2]
    down_terms = down_terms.reshape(mlp_count, width // piece, tok_dev, piece)
    down_sum = (
        lax.psum_scatter(down_terms, "mlp", scatter_dimension=0, tiled=True)[0]
        .transpose(1, 0, 2)
        .reshape(tok_dev, width)
        .astype(jnp.float32)
    )
    result = (values + gate_rows * down_sum).astype(jnp.bfloat16)
    return result.reshape(tok_dev, 1, width)


def solution(mesh):
    placed = (
        P("req", "mlp"),
        P("req", "mlp"),
        P(),
        P(),
        P(),
        P("mlp", "req"),
        P("mlp", None, None),
        P(None, None, "mlp"),
        P(),
        P("mlp", None, None),
        P(None, None, "mlp"),
        P("req", "mlp"),
        P("mlp", "req"),
    )
    return jax.shard_map(
        local, mesh=mesh, in_specs=placed, out_specs=P(None, "req", "mlp"), check_vma=False
    )
```

```python
import jax
import jax.numpy as jnp
from jax import lax
from jax.sharding import PartitionSpec as P

MODEL_WIDTH = 5120
ADAPTER_RANK = 16
ADAPTER_TOTAL = 16
TOK_DEV = 384
Y_COUNT = 4


norm_epsilon = 1e-06


def send_layout(packed, offset, req_count):
    shaped = packed.reshape(packed.shape[0] // req_count, req_count, packed.shape[1])
    return jnp.roll(shaped, offset, axis=1)


def compact(moved, starts, ends, req_count, token_rank):
    slots = moved.shape[0] * moved.shape[1]
    flat_rows = moved.reshape(slots, moved.shape[2])
    source = jnp.sum((ends[None, :] <= token_rank[:, None]).astype(jnp.int32), axis=1)
    source_hot = source[:, None] == jnp.arange(req_count, dtype=jnp.int32)[None, :]
    source_start = jnp.sum(jnp.where(source_hot, starts[None, :], 0), axis=1)
    position = (token_rank - source_start) // req_count * req_count + source
    return jnp.take(flat_rows, position, axis=0)


def token_groups(token_rank, request_length, request_group, adapter_per_group):
    req_ends = jnp.cumsum(request_length.reshape(-1))
    request_count = req_ends.shape[0]
    request = jnp.sum((req_ends[None, :] <= token_rank[:, None]).astype(jnp.int32), axis=1)
    request = jnp.minimum(request, request_count - 1)
    request_hot = request[:, None] == jnp.arange(request_count, dtype=jnp.int32)[None, :]
    group_ids = jnp.sum(jnp.where(request_hot, request_group[None, :], 0), axis=1)
    group_count = adapter_per_group.shape[0]
    group_hot = group_ids[:, None] == jnp.arange(group_count, dtype=jnp.int32)[None, :]
    adapter_of_row = jnp.sum(jnp.where(group_hot, adapter_per_group[None, :], 0), axis=1)
    adapter_hot = (
        adapter_of_row[:, None] == jnp.arange(ADAPTER_TOTAL, dtype=jnp.int32)[None, :]
    ).astype(jnp.float32)
    return group_ids, adapter_hot


def select_low(output_rank_rows, adapter_hot):
    shaped = output_rank_rows.reshape(output_rank_rows.shape[0], ADAPTER_TOTAL, ADAPTER_RANK)
    return jnp.sum(shaped * adapter_hot[:, :, None], axis=1)


def expand_rank_rows(low_rows, adapter_hot):
    spread_rows = adapter_hot.astype(jnp.bfloat16)[:, :, None] * low_rows[:, None, :]
    return spread_rows.reshape(low_rows.shape[0], ADAPTER_TOTAL * ADAPTER_RANK)


def mlp_sum(part):
    n = lax.axis_size("mlp")
    total = part.astype(jnp.float32)
    bit = 1
    while bit < n:
        total = total + lax.ppermute(total, "mlp", [(i, i ^ bit) for i in range(n)])
        bit *= 2
    return total


def mlp_move(block, target):
    n = lax.axis_size("mlp")
    return lax.ppermute(block, "mlp", [(i, target(i)) for i in range(n)])


def y_shift(step, y_count):
    return lambda i: ((i // 2 + step) % y_count) * 2 + i % 2


def scatter_mlp(payload):
    y_count = payload.shape[1]
    m = lax.axis_index("mlp")
    y_here = m // 2
    core = m % 2
    mine = lax.dynamic_index_in_dim(payload, core, 0, keepdims=False)
    other = lax.dynamic_index_in_dim(payload, 1 - core, 0, keepdims=False)
    pair = mine.astype(jnp.float32) + mlp_move(other, lambda i: i ^ 1).astype(jnp.float32)
    pair_b = pair.astype(jnp.bfloat16)
    total = lax.dynamic_index_in_dim(pair, y_here, 0, keepdims=False)
    for step in range(1, y_count):
        send = lax.dynamic_index_in_dim(pair_b, (y_here + step) % y_count, 0, keepdims=False)
        total = total + mlp_move(send, y_shift(step, y_count)).astype(jnp.float32)
    return total


def gather_mlp(block, y_count):
    m = lax.axis_index("mlp")
    y_here = m // 2
    core = m % 2
    pair = jnp.stack([block, mlp_move(block, lambda i: i ^ 1)], axis=0)
    rows = [pair] + [mlp_move(pair, y_shift(step, y_count)) for step in range(1, y_count)]
    held = jnp.stack(rows, axis=0).reshape((2 * y_count,) + block.shape)
    target = jnp.arange(2 * y_count, dtype=jnp.int32)
    slot = ((y_here - target // 2) % y_count) * 2 + (target % 2) ^ core
    return jnp.take(held, slot, axis=0)


def by_core(stack, y_count):
    rest = stack.shape[1:]
    shaped = stack.reshape((y_count, 2, 2) + rest)
    return jnp.swapaxes(shaped, 0, 1).reshape((2 * y_count * 2,) + rest)


def local(
    residual_input,
    attention_output,
    request_length,
    request_group,
    adapter_per_group,
    output_weight,
    output_down_maps,
    output_up_maps,
    modulation,
    hidden_down_maps,
    hidden_up_maps,
    up_weight,
    down_weight,
):
    req_count = lax.axis_size("req")
    mlp_count = lax.axis_size("mlp")
    device_index = lax.axis_index("req")
    column_index = lax.axis_index("mlp")
    width = residual_input.shape[1]
    head_width = attention_output.shape[1]

    out_w = by_core(lax.all_gather(output_weight, "req", axis=0, tiled=False), Y_COUNT)
    up_w = lax.all_gather(up_weight, "req", axis=0, tiled=True)
    down_w = by_core(lax.all_gather(down_weight, "req", axis=0, tiled=False), Y_COUNT)

    live_rows = jnp.sum(request_length, axis=1)
    dev_ends = jnp.cumsum(live_rows)
    dev_starts = dev_ends - live_rows
    offset = dev_starts[device_index]
    tok_dev = TOK_DEV
    token_rank = jnp.arange(tok_dev, dtype=jnp.int32) * req_count + device_index
    moved_attn = lax.all_to_all(
        send_layout(attention_output, offset, req_count), "req", split_axis=1, concat_axis=1, tiled=True
    )
    attention_rows = compact(moved_attn, dev_starts, dev_ends, req_count, token_rank)
    moved_res = lax.all_to_all(
        send_layout(residual_input, offset, req_count), "req", split_axis=1, concat_axis=1, tiled=True
    )
    residual_rows = compact(moved_res, dev_starts, dev_ends, req_count, token_rank)

    group_ids, adapter_hot = token_groups(token_rank, request_length, request_group, adapter_per_group)
    shift_rows = jnp.take(modulation[:, 0, :], group_ids, axis=0)
    scale_rows = jnp.take(modulation[:, 1, :], group_ids, axis=0)
    gate_table = lax.dynamic_slice_in_dim(modulation[:, 2, :], column_index * width, width, 1)
    gate_rows = jnp.take(gate_table, group_ids, axis=0)

    piece = out_w.shape[2]
    head_terms = jnp.einsum(
        "tk,rkc->rtc", attention_rows, out_w, preferred_element_type=jnp.float32
    ).reshape(2, Y_COUNT, width // piece * tok_dev, piece)
    out_low = select_low(
        jnp.dot(
            attention_rows,
            output_down_maps.reshape(head_width, ADAPTER_TOTAL * ADAPTER_RANK),
            preferred_element_type=jnp.float32,
        ),
        adapter_hot,
    )
    low_count = out_low.size
    low_rows = -(-low_count // piece)
    low_flat = jnp.pad(out_low.reshape(-1), (0, low_rows * piece - low_count)).reshape(
        1, 1, low_rows, piece
    )
    send = jnp.concatenate(
        [head_terms, jnp.broadcast_to(low_flat, (2, Y_COUNT, low_rows, piece))], axis=2
    ).astype(jnp.bfloat16)
    summed = scatter_mlp(send)
    projection_rows = (
        summed[: head_terms.shape[2]]
        .reshape(width // piece, tok_dev, piece)
        .transpose(1, 0, 2)
        .reshape(tok_dev, width)
    )
    output_rank_values = (
        summed[head_terms.shape[2] :]
        .reshape(-1)[:low_count]
        .reshape(tok_dev, ADAPTER_RANK)
        .astype(jnp.bfloat16)
    )
    adapter_delta = jnp.dot(
        expand_rank_rows(output_rank_values, adapter_hot),
        output_up_maps.reshape(ADAPTER_TOTAL * ADAPTER_RANK, width),
        preferred_element_type=jnp.float32,
    )
    blended_rows = (residual_rows.astype(jnp.float32) + projection_rows + adapter_delta).astype(
        jnp.bfloat16
    )
    values = blended_rows.astype(jnp.float32)

    full_rows = gather_mlp(blended_rows, Y_COUNT).astype(jnp.float32)
    row_mean = jnp.sum(full_rows, axis=(0, 2)) / MODEL_WIDTH
    variance = jnp.sum(full_rows * full_rows, axis=(0, 2)) / MODEL_WIDTH - row_mean * row_mean
    inv = lax.rsqrt(variance + norm_epsilon)
    scale_m = (1.0 + scale_rows).reshape(-1, mlp_count, width).transpose(1, 0, 2)
    shift_m = shift_rows.reshape(-1, mlp_count, width).transpose(1, 0, 2)
    normalized = (
        (full_rows - row_mean[None, :, None]) * inv[None, :, None] * scale_m + shift_m
    ).astype(jnp.bfloat16)

    normed_local = lax.dynamic_index_in_dim(normalized, column_index, 0, keepdims=False)
    part_low = jnp.dot(
        normed_local,
        hidden_down_maps.reshape(width, ADAPTER_TOTAL * ADAPTER_RANK),
        preferred_element_type=jnp.float32,
    )
    hidden_rank_values = mlp_sum(select_low(part_low, adapter_hot).astype(jnp.bfloat16)).astype(
        jnp.bfloat16
    )
    hidden_units = up_weight.shape[1]
    hidden_total = jnp.einsum(
        "mtc,mch->th",
        normalized,
        up_w.reshape(mlp_count, width, hidden_units),
        preferred_element_type=jnp.float32,
    )
    hidden_total = hidden_total + jnp.dot(
        expand_rank_rows(hidden_rank_values, adapter_hot),
        hidden_up_maps.reshape(ADAPTER_TOTAL * ADAPTER_RANK, hidden_units),
        preferred_element_type=jnp.float32,
    )
    hidden = jax.nn.gelu(hidden_total, approximate=True).astype(jnp.bfloat16)
    piece = down_w.shape[2]
    down_terms = jnp.einsum(
        "th,rhc->rtc", hidden, down_w, preferred_element_type=jnp.float32
    ).astype(jnp.bfloat16)
    down_sum = (
        scatter_mlp(down_terms.reshape(2, Y_COUNT, width // piece * tok_dev, piece))
        .reshape(width // piece, tok_dev, piece)
        .transpose(1, 0, 2)
        .reshape(tok_dev, width)
    )
    result = (values + gate_rows * down_sum).astype(jnp.bfloat16)
    return result.reshape(tok_dev, 1, width)


def solution(mesh):
    placed = (
        P("req", "mlp"),
        P("req", "mlp"),
        P(),
        P(),
        P(),
        P("mlp", "req"),
        P("mlp", None, None),
        P(None, None, "mlp"),
        P(),
        P("mlp", None, None),
        P(None, None, "mlp"),
        P("req", "mlp"),
        P("mlp", "req"),
    )
    return jax.shard_map(
        local, mesh=mesh, in_specs=placed, out_specs=P(None, "req", "mlp"), check_vma=False
    )
```

```python
import jax
import jax.numpy as jnp
from jax import lax
from jax.sharding import PartitionSpec as P

MODEL_WIDTH = 5120
ADAPTER_RANK = 16
ADAPTER_TOTAL = 16
TOK_DEV = 384
Y_COUNT = 4


norm_epsilon = 1e-06


def send_layout(packed, offset, req_count):
    shaped = packed.reshape(packed.shape[0] // req_count, req_count, packed.shape[1])
    return jnp.roll(shaped, offset, axis=1)


def compact(moved, starts, ends, req_count, token_rank):
    slots = moved.shape[0] * moved.shape[1]
    flat_rows = moved.reshape(slots, moved.shape[2])
    source = jnp.sum((ends[None, :] <= token_rank[:, None]).astype(jnp.int32), axis=1)
    source_hot = source[:, None] == jnp.arange(req_count, dtype=jnp.int32)[None, :]
    source_start = jnp.sum(jnp.where(source_hot, starts[None, :], 0), axis=1)
    position = (token_rank - source_start) // req_count * req_count + source
    return jnp.take(flat_rows, position, axis=0)


def token_groups(token_rank, request_length, request_group, adapter_per_group):
    req_ends = jnp.cumsum(request_length.reshape(-1))
    request_count = req_ends.shape[0]
    request = jnp.sum((req_ends[None, :] <= token_rank[:, None]).astype(jnp.int32), axis=1)
    request = jnp.minimum(request, request_count - 1)
    request_hot = request[:, None] == jnp.arange(request_count, dtype=jnp.int32)[None, :]
    group_ids = jnp.sum(jnp.where(request_hot, request_group[None, :], 0), axis=1)
    group_count = adapter_per_group.shape[0]
    group_hot = group_ids[:, None] == jnp.arange(group_count, dtype=jnp.int32)[None, :]
    adapter_of_row = jnp.sum(jnp.where(group_hot, adapter_per_group[None, :], 0), axis=1)
    adapter_hot = (
        adapter_of_row[:, None] == jnp.arange(ADAPTER_TOTAL, dtype=jnp.int32)[None, :]
    ).astype(jnp.float32)
    return group_ids, adapter_hot


def select_low(output_rank_rows, adapter_hot):
    shaped = output_rank_rows.reshape(output_rank_rows.shape[0], ADAPTER_TOTAL, ADAPTER_RANK)
    return jnp.sum(shaped * adapter_hot[:, :, None], axis=1)


def expand_rank_rows(low_rows, adapter_hot):
    spread_rows = adapter_hot.astype(jnp.bfloat16)[:, :, None] * low_rows[:, None, :]
    return spread_rows.reshape(low_rows.shape[0], ADAPTER_TOTAL * ADAPTER_RANK)


def mlp_sum(part):
    n = lax.axis_size("mlp")
    total = part.astype(jnp.float32)
    bit = 1
    while bit < n:
        total = total + lax.ppermute(total, "mlp", [(i, i ^ bit) for i in range(n)])
        bit *= 2
    return total


def mlp_move(block, target):
    n = lax.axis_size("mlp")
    return lax.ppermute(block, "mlp", [(i, target(i)) for i in range(n)])


def y_shift(step, y_count):
    return lambda i: ((i // 2 + step) % y_count) * 2 + i % 2


def scatter_mlp(payload):
    y_count = payload.shape[0]
    m = lax.axis_index("mlp")
    y_here = m // 2
    core = m % 2
    mine = lax.dynamic_index_in_dim(payload, core, 1, keepdims=False)
    other = lax.dynamic_index_in_dim(payload, 1 - core, 1, keepdims=False)
    pair = mine.astype(jnp.float32) + mlp_move(other, lambda i: i ^ 1).astype(jnp.float32)
    pair_b = pair.astype(jnp.bfloat16)
    total = lax.dynamic_index_in_dim(pair, y_here, 0, keepdims=False)
    for step in range(1, y_count):
        send = lax.dynamic_index_in_dim(pair_b, (y_here + step) % y_count, 0, keepdims=False)
        total = total + mlp_move(send, y_shift(step, y_count)).astype(jnp.float32)
    return total


def gather_mlp(block, y_count):
    m = lax.axis_index("mlp")
    y_here = m // 2
    core = m % 2
    pair = jnp.stack([block, mlp_move(block, lambda i: i ^ 1)], axis=0)
    rows = [pair] + [mlp_move(pair, y_shift(step, y_count)) for step in range(1, y_count)]
    held = jnp.stack(rows, axis=0).reshape((2 * y_count,) + block.shape)
    target = jnp.arange(2 * y_count, dtype=jnp.int32)
    slot = ((y_here - target // 2) % y_count) * 2 + (target % 2) ^ core
    return jnp.take(held, slot, axis=0)


def local(
    residual_input,
    attention_output,
    request_length,
    request_group,
    adapter_per_group,
    output_weight,
    output_down_maps,
    output_up_maps,
    modulation,
    hidden_down_maps,
    hidden_up_maps,
    up_weight,
    down_weight,
):
    req_count = lax.axis_size("req")
    mlp_count = lax.axis_size("mlp")
    device_index = lax.axis_index("req")
    column_index = lax.axis_index("mlp")
    width = residual_input.shape[1]
    head_width = attention_output.shape[1]

    out_w = lax.all_gather(output_weight, "req", axis=1, tiled=True)
    up_w = lax.all_gather(up_weight, "req", axis=0, tiled=True)
    down_w = lax.all_gather(down_weight, "req", axis=1, tiled=True)

    live_rows = jnp.sum(request_length, axis=1)
    dev_ends = jnp.cumsum(live_rows)
    dev_starts = dev_ends - live_rows
    offset = dev_starts[device_index]
    tok_dev = TOK_DEV
    token_rank = jnp.arange(tok_dev, dtype=jnp.int32) * req_count + device_index
    moved_attn = lax.all_to_all(
        send_layout(attention_output, offset, req_count), "req", split_axis=1, concat_axis=1, tiled=True
    )
    attention_rows = compact(moved_attn, dev_starts, dev_ends, req_count, token_rank)
    moved_res = lax.all_to_all(
        send_layout(residual_input, offset, req_count), "req", split_axis=1, concat_axis=1, tiled=True
    )
    residual_rows = compact(moved_res, dev_starts, dev_ends, req_count, token_rank)

    group_ids, adapter_hot = token_groups(token_rank, request_length, request_group, adapter_per_group)
    shift_rows = jnp.take(modulation[:, 0, :], group_ids, axis=0)
    scale_rows = jnp.take(modulation[:, 1, :], group_ids, axis=0)
    gate_table = lax.dynamic_slice_in_dim(modulation[:, 2, :], column_index * width, width, 1)
    gate_rows = jnp.take(gate_table, group_ids, axis=0)

    head_terms = jnp.einsum(
        "tk,kmc->mtc",
        attention_rows,
        out_w.reshape(head_width, mlp_count, width),
        preferred_element_type=jnp.float32,
    )
    out_low = select_low(
        jnp.dot(
            attention_rows,
            output_down_maps.reshape(head_width, ADAPTER_TOTAL * ADAPTER_RANK),
            preferred_element_type=jnp.float32,
        ),
        adapter_hot,
    )
    low_count = out_low.size
    low_rows = -(-low_count // width)
    low_flat = jnp.pad(out_low.reshape(-1), (0, low_rows * width - low_count)).reshape(
        1, low_rows, width
    )
    send = jnp.concatenate(
        [head_terms, jnp.broadcast_to(low_flat, (mlp_count, low_rows, width))], axis=1
    ).astype(jnp.bfloat16)
    summed = scatter_mlp(send.reshape((Y_COUNT, mlp_count // Y_COUNT) + send.shape[1:]))
    projection_rows = summed[:tok_dev]
    output_rank_values = (
        summed[tok_dev:].reshape(-1)[:low_count].reshape(tok_dev, ADAPTER_RANK).astype(jnp.bfloat16)
    )
    adapter_delta = jnp.dot(
        expand_rank_rows(output_rank_values, adapter_hot),
        output_up_maps.reshape(ADAPTER_TOTAL * ADAPTER_RANK, width),
        preferred_element_type=jnp.float32,
    )
    blended_rows = (residual_rows.astype(jnp.float32) + projection_rows + adapter_delta).astype(
        jnp.bfloat16
    )
    values = blended_rows.astype(jnp.float32)

    full_rows = gather_mlp(blended_rows, Y_COUNT).astype(jnp.float32)
    row_mean = jnp.sum(full_rows, axis=(0, 2)) / MODEL_WIDTH
    variance = jnp.sum(full_rows * full_rows, axis=(0, 2)) / MODEL_WIDTH - row_mean * row_mean
    inv = lax.rsqrt(variance + norm_epsilon)
    scale_m = (1.0 + scale_rows).reshape(-1, mlp_count, width).transpose(1, 0, 2)
    shift_m = shift_rows.reshape(-1, mlp_count, width).transpose(1, 0, 2)
    normalized = (
        (full_rows - row_mean[None, :, None]) * inv[None, :, None] * scale_m + shift_m
    ).astype(jnp.bfloat16)

    normed_local = lax.dynamic_index_in_dim(normalized, column_index, 0, keepdims=False)
    part_low = jnp.dot(
        normed_local,
        hidden_down_maps.reshape(width, ADAPTER_TOTAL * ADAPTER_RANK),
        preferred_element_type=jnp.float32,
    )
    hidden_rank_values = mlp_sum(select_low(part_low, adapter_hot).astype(jnp.bfloat16)).astype(
        jnp.bfloat16
    )
    hidden_units = up_weight.shape[1]
    hidden_total = jnp.einsum(
        "mtc,mch->th",
        normalized,
        up_w.reshape(mlp_count, width, hidden_units),
        preferred_element_type=jnp.float32,
    )
    hidden_total = hidden_total + jnp.dot(
        expand_rank_rows(hidden_rank_values, adapter_hot),
        hidden_up_maps.reshape(ADAPTER_TOTAL * ADAPTER_RANK, hidden_units),
        preferred_element_type=jnp.float32,
    )
    hidden = jax.nn.gelu(hidden_total, approximate=True).astype(jnp.bfloat16)
    down_terms = jnp.einsum(
        "th,hmc->mtc",
        hidden,
        down_w.reshape(hidden_units, mlp_count, width),
        preferred_element_type=jnp.float32,
    ).astype(jnp.bfloat16)
    down_sum = scatter_mlp(
        down_terms.reshape((Y_COUNT, mlp_count // Y_COUNT) + down_terms.shape[1:])
    )
    result = (values + gate_rows * down_sum).astype(jnp.bfloat16)
    return result.reshape(tok_dev, 1, width)


def solution(mesh):
    placed = (
        P("req", "mlp"),
        P("req", "mlp"),
        P(),
        P(),
        P(),
        P("mlp", "req"),
        P("mlp", None, None),
        P(None, None, "mlp"),
        P(),
        P("mlp", None, None),
        P(None, None, "mlp"),
        P("req", "mlp"),
        P("mlp", "req"),
    )
    return jax.shard_map(
        local, mesh=mesh, in_specs=placed, out_specs=P(None, "req", "mlp"), check_vma=False
    )
```

```python
import jax
import jax.numpy as jnp
from jax import lax
from jax.sharding import PartitionSpec as P

MODEL_WIDTH = 5120
ADAPTER_RANK = 16
ADAPTER_TOTAL = 16
TOK_DEV = 384
Y_COUNT = 4


norm_epsilon = 1e-06


def send_layout(packed, offset, req_count):
    shaped = packed.reshape(packed.shape[0] // req_count, req_count, packed.shape[1])
    return jnp.roll(shaped, offset, axis=1)


def compact(moved, starts, ends, req_count, token_rank):
    slots = moved.shape[0] * moved.shape[1]
    flat_rows = moved.reshape(slots, moved.shape[2])
    source = jnp.sum((ends[None, :] <= token_rank[:, None]).astype(jnp.int32), axis=1)
    source_hot = source[:, None] == jnp.arange(req_count, dtype=jnp.int32)[None, :]
    source_start = jnp.sum(jnp.where(source_hot, starts[None, :], 0), axis=1)
    position = (token_rank - source_start) // req_count * req_count + source
    return jnp.take(flat_rows, position, axis=0)


def token_groups(token_rank, request_length, request_group, adapter_per_group):
    req_ends = jnp.cumsum(request_length.reshape(-1))
    request_count = req_ends.shape[0]
    request = jnp.sum((req_ends[None, :] <= token_rank[:, None]).astype(jnp.int32), axis=1)
    request = jnp.minimum(request, request_count - 1)
    request_hot = request[:, None] == jnp.arange(request_count, dtype=jnp.int32)[None, :]
    group_ids = jnp.sum(jnp.where(request_hot, request_group[None, :], 0), axis=1)
    group_count = adapter_per_group.shape[0]
    group_hot = group_ids[:, None] == jnp.arange(group_count, dtype=jnp.int32)[None, :]
    adapter_of_row = jnp.sum(jnp.where(group_hot, adapter_per_group[None, :], 0), axis=1)
    adapter_hot = (
        adapter_of_row[:, None] == jnp.arange(ADAPTER_TOTAL, dtype=jnp.int32)[None, :]
    ).astype(jnp.float32)
    return group_ids, adapter_hot


def select_low(output_rank_rows, adapter_hot):
    shaped = output_rank_rows.reshape(output_rank_rows.shape[0], ADAPTER_TOTAL, ADAPTER_RANK)
    return jnp.sum(shaped * adapter_hot[:, :, None], axis=1)


def expand_rank_rows(low_rows, adapter_hot):
    spread_rows = adapter_hot.astype(jnp.bfloat16)[:, :, None] * low_rows[:, None, :]
    return spread_rows.reshape(low_rows.shape[0], ADAPTER_TOTAL * ADAPTER_RANK)


def mlp_sum(part):
    n = lax.axis_size("mlp")
    total = part.astype(jnp.float32)
    bit = 1
    while bit < n:
        total = total + lax.ppermute(total, "mlp", [(i, i ^ bit) for i in range(n)])
        bit *= 2
    return total


def mlp_move(block, target):
    n = lax.axis_size("mlp")
    return lax.ppermute(block, "mlp", [(i, target(i)) for i in range(n)])


def y_shift(step, y_count):
    return lambda i: ((i // 2 + step) % y_count) * 2 + i % 2


def scatter_mlp(payload):
    y_count = payload.shape[0]
    m = lax.axis_index("mlp")
    y_here = m // 2
    core = m % 2
    mine = lax.dynamic_index_in_dim(payload, core, 1, keepdims=False)
    other = lax.dynamic_index_in_dim(payload, 1 - core, 1, keepdims=False)
    pair = mine.astype(jnp.float32) + mlp_move(other, lambda i: i ^ 1).astype(jnp.float32)
    pair_b = pair.astype(jnp.bfloat16)
    total = lax.dynamic_index_in_dim(pair, y_here, 0, keepdims=False)
    for step in range(1, y_count):
        send = lax.dynamic_index_in_dim(pair_b, (y_here + step) % y_count, 0, keepdims=False)
        total = total + mlp_move(send, y_shift(step, y_count)).astype(jnp.float32)
    return total


def gather_mlp(block, y_count):
    m = lax.axis_index("mlp")
    y_here = m // 2
    core = m % 2
    pair = jnp.stack([block, mlp_move(block, lambda i: i ^ 1)], axis=0)
    rows = [pair] + [mlp_move(pair, y_shift(step, y_count)) for step in range(1, y_count)]
    held = jnp.stack(rows, axis=0).reshape((2 * y_count,) + block.shape)
    target = jnp.arange(2 * y_count, dtype=jnp.int32)
    slot = ((y_here - target // 2) % y_count) * 2 + (target % 2) ^ core
    return jnp.take(held, slot, axis=0)


def local(
    residual_input,
    attention_output,
    request_length,
    request_group,
    adapter_per_group,
    output_weight,
    output_down_maps,
    output_up_maps,
    modulation,
    hidden_down_maps,
    hidden_up_maps,
    up_weight,
    down_weight,
):
    req_count = lax.axis_size("req")
    mlp_count = lax.axis_size("mlp")
    device_index = lax.axis_index("req")
    column_index = lax.axis_index("mlp")
    width = residual_input.shape[1]
    head_width = attention_output.shape[1]

    out_w = lax.all_gather(output_weight, "req", axis=1, tiled=True)
    up_w = lax.all_gather(up_weight, "req", axis=0, tiled=True)
    split = down_weight.shape[1] // 2
    down_halves = [
        lax.all_gather(down_weight[:, :split], "req", axis=1, tiled=True),
        lax.all_gather(down_weight[:, split:], "req", axis=1, tiled=True),
    ]

    live_rows = jnp.sum(request_length, axis=1)
    dev_ends = jnp.cumsum(live_rows)
    dev_starts = dev_ends - live_rows
    offset = dev_starts[device_index]
    tok_dev = TOK_DEV
    token_rank = jnp.arange(tok_dev, dtype=jnp.int32) * req_count + device_index
    moved_attn = lax.all_to_all(
        send_layout(attention_output, offset, req_count), "req", split_axis=1, concat_axis=1, tiled=True
    )
    attention_rows = compact(moved_attn, dev_starts, dev_ends, req_count, token_rank)
    moved_res = lax.all_to_all(
        send_layout(residual_input, offset, req_count), "req", split_axis=1, concat_axis=1, tiled=True
    )
    residual_rows = compact(moved_res, dev_starts, dev_ends, req_count, token_rank)

    group_ids, adapter_hot = token_groups(token_rank, request_length, request_group, adapter_per_group)
    shift_rows = jnp.take(modulation[:, 0, :], group_ids, axis=0)
    scale_rows = jnp.take(modulation[:, 1, :], group_ids, axis=0)
    gate_table = lax.dynamic_slice_in_dim(modulation[:, 2, :], column_index * width, width, 1)
    gate_rows = jnp.take(gate_table, group_ids, axis=0)

    head_terms = jnp.einsum(
        "tk,kmc->mtc",
        attention_rows,
        out_w.reshape(head_width, mlp_count, width),
        preferred_element_type=jnp.float32,
    )
    out_low = select_low(
        jnp.dot(
            attention_rows,
            output_down_maps.reshape(head_width, ADAPTER_TOTAL * ADAPTER_RANK),
            preferred_element_type=jnp.float32,
        ),
        adapter_hot,
    )
    low_count = out_low.size
    low_rows = -(-low_count // width)
    low_flat = jnp.pad(out_low.reshape(-1), (0, low_rows * width - low_count)).reshape(
        1, low_rows, width
    )
    send = jnp.concatenate(
        [head_terms, jnp.broadcast_to(low_flat, (mlp_count, low_rows, width))], axis=1
    ).astype(jnp.bfloat16)
    summed = scatter_mlp(send.reshape((Y_COUNT, mlp_count // Y_COUNT) + send.shape[1:]))
    projection_rows = summed[:tok_dev]
    output_rank_values = (
        summed[tok_dev:].reshape(-1)[:low_count].reshape(tok_dev, ADAPTER_RANK).astype(jnp.bfloat16)
    )
    adapter_delta = jnp.dot(
        expand_rank_rows(output_rank_values, adapter_hot),
        output_up_maps.reshape(ADAPTER_TOTAL * ADAPTER_RANK, width),
        preferred_element_type=jnp.float32,
    )
    blended_rows = (residual_rows.astype(jnp.float32) + projection_rows + adapter_delta).astype(
        jnp.bfloat16
    )
    values = blended_rows.astype(jnp.float32)

    full_rows = gather_mlp(blended_rows, Y_COUNT).astype(jnp.float32)
    row_mean = jnp.sum(full_rows, axis=(0, 2)) / MODEL_WIDTH
    variance = jnp.sum(full_rows * full_rows, axis=(0, 2)) / MODEL_WIDTH - row_mean * row_mean
    inv = lax.rsqrt(variance + norm_epsilon)
    scale_m = (1.0 + scale_rows).reshape(-1, mlp_count, width).transpose(1, 0, 2)
    shift_m = shift_rows.reshape(-1, mlp_count, width).transpose(1, 0, 2)
    normalized = (
        (full_rows - row_mean[None, :, None]) * inv[None, :, None] * scale_m + shift_m
    ).astype(jnp.bfloat16)

    normed_local = lax.dynamic_index_in_dim(normalized, column_index, 0, keepdims=False)
    part_low = jnp.dot(
        normed_local,
        hidden_down_maps.reshape(width, ADAPTER_TOTAL * ADAPTER_RANK),
        preferred_element_type=jnp.float32,
    )
    hidden_rank_values = mlp_sum(select_low(part_low, adapter_hot).astype(jnp.bfloat16)).astype(
        jnp.bfloat16
    )
    hidden_units = up_weight.shape[1]
    hidden_total = jnp.einsum(
        "mtc,mch->th",
        normalized,
        up_w.reshape(mlp_count, width, hidden_units),
        preferred_element_type=jnp.float32,
    )
    hidden_total = hidden_total + jnp.dot(
        expand_rank_rows(hidden_rank_values, adapter_hot),
        hidden_up_maps.reshape(ADAPTER_TOTAL * ADAPTER_RANK, hidden_units),
        preferred_element_type=jnp.float32,
    )
    hidden = jax.nn.gelu(hidden_total, approximate=True).astype(jnp.bfloat16)
    sums = []
    for index in range(len(down_halves)):
        down_half = down_halves[index]
        if sums:
            sums[-1], down_half = lax.optimization_barrier((sums[-1], down_half))
        down_terms = jnp.einsum(
            "th,hmjc->mtjc",
            hidden,
            down_half.reshape(hidden_units, mlp_count, 2, split),
            preferred_element_type=jnp.float32,
        ).astype(jnp.bfloat16)
        sums.append(
            scatter_mlp(down_terms.reshape((Y_COUNT, mlp_count // Y_COUNT) + down_terms.shape[1:]))
        )
    down_sum = jnp.concatenate(sums, axis=-1).reshape(tok_dev, width)
    result = (values + gate_rows * down_sum).astype(jnp.bfloat16)
    return result.reshape(tok_dev, 1, width)


def solution(mesh):
    placed = (
        P("req", "mlp"),
        P("req", "mlp"),
        P(),
        P(),
        P(),
        P("mlp", "req"),
        P("mlp", None, None),
        P(None, None, "mlp"),
        P(),
        P("mlp", None, None),
        P(None, None, "mlp"),
        P("req", "mlp"),
        P("mlp", "req"),
    )
    return jax.shard_map(
        local, mesh=mesh, in_specs=placed, out_specs=P(None, "req", "mlp"), check_vma=False
    )
```

```python
import jax
import jax.numpy as jnp
from jax import lax
from jax.sharding import PartitionSpec as P

MODEL_WIDTH = 5120
ADAPTER_RANK = 16
ADAPTER_TOTAL = 16
TOK_DEV = 384
Y_COUNT = 4


norm_epsilon = 1e-06


def send_layout(packed, offset, req_count):
    shaped = packed.reshape(packed.shape[0] // req_count, req_count, packed.shape[1])
    return jnp.roll(shaped, offset, axis=1)


def compact(moved, starts, ends, req_count, token_rank):
    slots = moved.shape[0] * moved.shape[1]
    flat_rows = moved.reshape(slots, moved.shape[2])
    source = jnp.sum((ends[None, :] <= token_rank[:, None]).astype(jnp.int32), axis=1)
    source_hot = source[:, None] == jnp.arange(req_count, dtype=jnp.int32)[None, :]
    source_start = jnp.sum(jnp.where(source_hot, starts[None, :], 0), axis=1)
    position = (token_rank - source_start) // req_count * req_count + source
    return jnp.take(flat_rows, position, axis=0)


def token_groups(token_rank, request_length, request_group, adapter_per_group):
    req_ends = jnp.cumsum(request_length.reshape(-1))
    request_count = req_ends.shape[0]
    request = jnp.sum((req_ends[None, :] <= token_rank[:, None]).astype(jnp.int32), axis=1)
    request = jnp.minimum(request, request_count - 1)
    request_hot = request[:, None] == jnp.arange(request_count, dtype=jnp.int32)[None, :]
    group_ids = jnp.sum(jnp.where(request_hot, request_group[None, :], 0), axis=1)
    group_count = adapter_per_group.shape[0]
    group_hot = group_ids[:, None] == jnp.arange(group_count, dtype=jnp.int32)[None, :]
    adapter_of_row = jnp.sum(jnp.where(group_hot, adapter_per_group[None, :], 0), axis=1)
    adapter_hot = (
        adapter_of_row[:, None] == jnp.arange(ADAPTER_TOTAL, dtype=jnp.int32)[None, :]
    ).astype(jnp.float32)
    return group_ids, adapter_hot


def select_low(output_rank_rows, adapter_hot):
    shaped = output_rank_rows.reshape(output_rank_rows.shape[0], ADAPTER_TOTAL, ADAPTER_RANK)
    return jnp.sum(shaped * adapter_hot[:, :, None], axis=1)


def expand_rank_rows(low_rows, adapter_hot):
    spread_rows = adapter_hot.astype(jnp.bfloat16)[:, :, None] * low_rows[:, None, :]
    return spread_rows.reshape(low_rows.shape[0], ADAPTER_TOTAL * ADAPTER_RANK)


def mlp_sum(part):
    n = lax.axis_size("mlp")
    total = part.astype(jnp.float32)
    bit = 1
    while bit < n:
        total = total + lax.ppermute(total, "mlp", [(i, i ^ bit) for i in range(n)])
        bit *= 2
    return total


def mlp_move(block, target):
    n = lax.axis_size("mlp")
    return lax.ppermute(block, "mlp", [(i, target(i)) for i in range(n)])


def y_shift(step, y_count):
    return lambda i: ((i // 2 + step) % y_count) * 2 + i % 2


def scatter_mlp(payload):
    y_count = payload.shape[0]
    m = lax.axis_index("mlp")
    y_here = m // 2
    core = m % 2
    mine = lax.dynamic_index_in_dim(payload, core, 1, keepdims=False)
    other = lax.dynamic_index_in_dim(payload, 1 - core, 1, keepdims=False)
    pair = mine.astype(jnp.float32) + mlp_move(other, lambda i: i ^ 1).astype(jnp.float32)
    pair_b = pair.astype(jnp.bfloat16)
    total = lax.dynamic_index_in_dim(pair, y_here, 0, keepdims=False)
    for step in range(1, y_count):
        send = lax.dynamic_index_in_dim(pair_b, (y_here + step) % y_count, 0, keepdims=False)
        total = total + mlp_move(send, y_shift(step, y_count)).astype(jnp.float32)
    return total


def gather_mlp(block, y_count):
    m = lax.axis_index("mlp")
    y_here = m // 2
    core = m % 2
    pair = jnp.stack([block, mlp_move(block, lambda i: i ^ 1)], axis=0)
    rows = [pair] + [mlp_move(pair, y_shift(step, y_count)) for step in range(1, y_count)]
    held = jnp.stack(rows, axis=0).reshape((2 * y_count,) + block.shape)
    target = jnp.arange(2 * y_count, dtype=jnp.int32)
    slot = ((y_here - target // 2) % y_count) * 2 + (target % 2) ^ core
    return jnp.take(held, slot, axis=0)


def local(
    residual_input,
    attention_output,
    request_length,
    request_group,
    adapter_per_group,
    output_weight,
    output_down_maps,
    output_up_maps,
    modulation,
    hidden_down_maps,
    hidden_up_maps,
    up_weight,
    down_weight,
):
    req_count = lax.axis_size("req")
    mlp_count = lax.axis_size("mlp")
    device_index = lax.axis_index("req")
    column_index = lax.axis_index("mlp")
    width = residual_input.shape[1]
    head_width = attention_output.shape[1]

    out_w = lax.all_gather(output_weight, "req", axis=1, tiled=True)
    up_size = up_weight.size
    lanes = 128
    both = jnp.concatenate([up_weight.reshape(-1), down_weight.reshape(-1)]).reshape(-1, lanes)
    both = lax.all_gather(both, "req", axis=0, tiled=False)
    up_w = both[:, : up_size // lanes].reshape((req_count * up_weight.shape[0],) + up_weight.shape[1:])
    down_w = (
        both[:, up_size // lanes :]
        .reshape((req_count,) + down_weight.shape)
        .transpose(1, 0, 2)
        .reshape(down_weight.shape[0], req_count * down_weight.shape[1])
    )

    live_rows = jnp.sum(request_length, axis=1)
    dev_ends = jnp.cumsum(live_rows)
    dev_starts = dev_ends - live_rows
    offset = dev_starts[device_index]
    tok_dev = TOK_DEV
    token_rank = jnp.arange(tok_dev, dtype=jnp.int32) * req_count + device_index
    moved_attn = lax.all_to_all(
        send_layout(attention_output, offset, req_count), "req", split_axis=1, concat_axis=1, tiled=True
    )
    attention_rows = compact(moved_attn, dev_starts, dev_ends, req_count, token_rank)
    moved_res = lax.all_to_all(
        send_layout(residual_input, offset, req_count), "req", split_axis=1, concat_axis=1, tiled=True
    )
    residual_rows = compact(moved_res, dev_starts, dev_ends, req_count, token_rank)

    group_ids, adapter_hot = token_groups(token_rank, request_length, request_group, adapter_per_group)
    shift_rows = jnp.take(modulation[:, 0, :], group_ids, axis=0)
    scale_rows = jnp.take(modulation[:, 1, :], group_ids, axis=0)
    gate_table = lax.dynamic_slice_in_dim(modulation[:, 2, :], column_index * width, width, 1)
    gate_rows = jnp.take(gate_table, group_ids, axis=0)

    head_terms = jnp.einsum(
        "tk,kmc->mtc",
        attention_rows,
        out_w.reshape(head_width, mlp_count, width),
        preferred_element_type=jnp.float32,
    )
    out_low = select_low(
        jnp.dot(
            attention_rows,
            output_down_maps.reshape(head_width, ADAPTER_TOTAL * ADAPTER_RANK),
            preferred_element_type=jnp.float32,
        ),
        adapter_hot,
    )
    low_count = out_low.size
    low_rows = -(-low_count // width)
    low_flat = jnp.pad(out_low.reshape(-1), (0, low_rows * width - low_count)).reshape(
        1, low_rows, width
    )
    send = jnp.concatenate(
        [head_terms, jnp.broadcast_to(low_flat, (mlp_count, low_rows, width))], axis=1
    ).astype(jnp.bfloat16)
    summed = scatter_mlp(send.reshape((Y_COUNT, mlp_count // Y_COUNT) + send.shape[1:]))
    projection_rows = summed[:tok_dev]
    output_rank_values = (
        summed[tok_dev:].reshape(-1)[:low_count].reshape(tok_dev, ADAPTER_RANK).astype(jnp.bfloat16)
    )
    adapter_delta = jnp.dot(
        expand_rank_rows(output_rank_values, adapter_hot),
        output_up_maps.reshape(ADAPTER_TOTAL * ADAPTER_RANK, width),
        preferred_element_type=jnp.float32,
    )
    blended_rows = (residual_rows.astype(jnp.float32) + projection_rows + adapter_delta).astype(
        jnp.bfloat16
    )
    values = blended_rows.astype(jnp.float32)

    full_rows = gather_mlp(blended_rows, Y_COUNT).astype(jnp.float32)
    row_mean = jnp.sum(full_rows, axis=(0, 2)) / MODEL_WIDTH
    variance = jnp.sum(full_rows * full_rows, axis=(0, 2)) / MODEL_WIDTH - row_mean * row_mean
    inv = lax.rsqrt(variance + norm_epsilon)
    scale_m = (1.0 + scale_rows).reshape(-1, mlp_count, width).transpose(1, 0, 2)
    shift_m = shift_rows.reshape(-1, mlp_count, width).transpose(1, 0, 2)
    normalized = (
        (full_rows - row_mean[None, :, None]) * inv[None, :, None] * scale_m + shift_m
    ).astype(jnp.bfloat16)

    normed_local = lax.dynamic_index_in_dim(normalized, column_index, 0, keepdims=False)
    part_low = jnp.dot(
        normed_local,
        hidden_down_maps.reshape(width, ADAPTER_TOTAL * ADAPTER_RANK),
        preferred_element_type=jnp.float32,
    )
    hidden_rank_values = mlp_sum(select_low(part_low, adapter_hot).astype(jnp.bfloat16)).astype(
        jnp.bfloat16
    )
    hidden_units = up_weight.shape[1]
    hidden_total = jnp.einsum(
        "mtc,mch->th",
        normalized,
        up_w.reshape(mlp_count, width, hidden_units),
        preferred_element_type=jnp.float32,
    )
    hidden_total = hidden_total + jnp.dot(
        expand_rank_rows(hidden_rank_values, adapter_hot),
        hidden_up_maps.reshape(ADAPTER_TOTAL * ADAPTER_RANK, hidden_units),
        preferred_element_type=jnp.float32,
    )
    hidden = jax.nn.gelu(hidden_total, approximate=True).astype(jnp.bfloat16)
    down_terms = jnp.einsum(
        "th,hmc->mtc",
        hidden,
        down_w.reshape(hidden_units, mlp_count, width),
        preferred_element_type=jnp.float32,
    ).astype(jnp.bfloat16)
    down_sum = scatter_mlp(
        down_terms.reshape((Y_COUNT, mlp_count // Y_COUNT) + down_terms.shape[1:])
    )
    result = (values + gate_rows * down_sum).astype(jnp.bfloat16)
    return result.reshape(tok_dev, 1, width)


def solution(mesh):
    placed = (
        P("req", "mlp"),
        P("req", "mlp"),
        P(),
        P(),
        P(),
        P("mlp", "req"),
        P("mlp", None, None),
        P(None, None, "mlp"),
        P(),
        P("mlp", None, None),
        P(None, None, "mlp"),
        P("req", "mlp"),
        P("mlp", "req"),
    )
    return jax.shard_map(
        local, mesh=mesh, in_specs=placed, out_specs=P(None, "req", "mlp"), check_vma=False
    )
```

```python
import jax
import jax.numpy as jnp
from jax import lax
from jax.sharding import PartitionSpec as P

MODEL_WIDTH = 5120
ADAPTER_RANK = 16
ADAPTER_TOTAL = 16
TOK_DEV = 384
Y_COUNT = 4


norm_epsilon = 1e-06


def send_layout(packed, offset, req_count):
    shaped = packed.reshape(packed.shape[0] // req_count, req_count, packed.shape[1])
    return jnp.roll(shaped, offset, axis=1)


def compact(moved, starts, ends, req_count, token_rank):
    slots = moved.shape[0] * moved.shape[1]
    flat_rows = moved.reshape(slots, moved.shape[2])
    source = jnp.sum((ends[None, :] <= token_rank[:, None]).astype(jnp.int32), axis=1)
    source_hot = source[:, None] == jnp.arange(req_count, dtype=jnp.int32)[None, :]
    source_start = jnp.sum(jnp.where(source_hot, starts[None, :], 0), axis=1)
    position = (token_rank - source_start) // req_count * req_count + source
    return jnp.take(flat_rows, position, axis=0)


def token_groups(token_rank, request_length, request_group, adapter_per_group):
    req_ends = jnp.cumsum(request_length.reshape(-1))
    request_count = req_ends.shape[0]
    request = jnp.sum((req_ends[None, :] <= token_rank[:, None]).astype(jnp.int32), axis=1)
    request = jnp.minimum(request, request_count - 1)
    request_hot = request[:, None] == jnp.arange(request_count, dtype=jnp.int32)[None, :]
    group_ids = jnp.sum(jnp.where(request_hot, request_group[None, :], 0), axis=1)
    group_count = adapter_per_group.shape[0]
    group_hot = group_ids[:, None] == jnp.arange(group_count, dtype=jnp.int32)[None, :]
    adapter_of_row = jnp.sum(jnp.where(group_hot, adapter_per_group[None, :], 0), axis=1)
    adapter_hot = (
        adapter_of_row[:, None] == jnp.arange(ADAPTER_TOTAL, dtype=jnp.int32)[None, :]
    ).astype(jnp.float32)
    return group_ids, adapter_hot


def select_low(output_rank_rows, adapter_hot):
    shaped = output_rank_rows.reshape(output_rank_rows.shape[0], ADAPTER_TOTAL, ADAPTER_RANK)
    return jnp.sum(shaped * adapter_hot[:, :, None], axis=1)


def expand_rank_rows(low_rows, adapter_hot):
    spread_rows = adapter_hot.astype(jnp.bfloat16)[:, :, None] * low_rows[:, None, :]
    return spread_rows.reshape(low_rows.shape[0], ADAPTER_TOTAL * ADAPTER_RANK)


def mlp_sum(part):
    n = lax.axis_size("mlp")
    total = part.astype(jnp.float32)
    bit = 1
    while bit < n:
        total = total + lax.ppermute(total, "mlp", [(i, i ^ bit) for i in range(n)])
        bit *= 2
    return total


def mlp_move(block, target):
    n = lax.axis_size("mlp")
    return lax.ppermute(block, "mlp", [(i, target(i)) for i in range(n)])


def y_shift(step, y_count):
    return lambda i: ((i // 2 + step) % y_count) * 2 + i % 2


def scatter_mlp(payload):
    y_count = payload.shape[0]
    m = lax.axis_index("mlp")
    y_here = m // 2
    core = m % 2
    mine = lax.dynamic_index_in_dim(payload, core, 1, keepdims=False)
    other = lax.dynamic_index_in_dim(payload, 1 - core, 1, keepdims=False)
    pair = mine.astype(jnp.float32) + mlp_move(other, lambda i: i ^ 1).astype(jnp.float32)
    pair_b = pair.astype(jnp.bfloat16)
    total = lax.dynamic_index_in_dim(pair, y_here, 0, keepdims=False)
    for step in range(1, y_count):
        send = lax.dynamic_index_in_dim(pair_b, (y_here + step) % y_count, 0, keepdims=False)
        total = total + mlp_move(send, y_shift(step, y_count)).astype(jnp.float32)
    return total


def gather_mlp(block, y_count):
    m = lax.axis_index("mlp")
    y_here = m // 2
    core = m % 2
    pair = jnp.stack([block, mlp_move(block, lambda i: i ^ 1)], axis=0)
    rows = [pair] + [mlp_move(pair, y_shift(step, y_count)) for step in range(1, y_count)]
    held = jnp.stack(rows, axis=0).reshape((2 * y_count,) + block.shape)
    target = jnp.arange(2 * y_count, dtype=jnp.int32)
    slot = ((y_here - target // 2) % y_count) * 2 + (target % 2) ^ core
    return jnp.take(held, slot, axis=0)


def local(
    residual_input,
    attention_output,
    request_length,
    request_group,
    adapter_per_group,
    output_weight,
    output_down_maps,
    output_up_maps,
    modulation,
    hidden_down_maps,
    hidden_up_maps,
    up_weight,
    down_weight,
):
    req_count = lax.axis_size("req")
    mlp_count = lax.axis_size("mlp")
    device_index = lax.axis_index("req")
    column_index = lax.axis_index("mlp")
    width = residual_input.shape[1]
    head_width = attention_output.shape[1]

    out_w = lax.all_gather(output_weight, "req", axis=1, tiled=True)
    both = jnp.stack([up_weight, down_weight.T], axis=0)
    both = lax.all_gather(both, "req", axis=1, tiled=True)
    up_w = both[0]
    down_t = both[1]

    live_rows = jnp.sum(request_length, axis=1)
    dev_ends = jnp.cumsum(live_rows)
    dev_starts = dev_ends - live_rows
    offset = dev_starts[device_index]
    tok_dev = TOK_DEV
    token_rank = jnp.arange(tok_dev, dtype=jnp.int32) * req_count + device_index
    moved_attn = lax.all_to_all(
        send_layout(attention_output, offset, req_count), "req", split_axis=1, concat_axis=1, tiled=True
    )
    attention_rows = compact(moved_attn, dev_starts, dev_ends, req_count, token_rank)
    moved_res = lax.all_to_all(
        send_layout(residual_input, offset, req_count), "req", split_axis=1, concat_axis=1, tiled=True
    )
    residual_rows = compact(moved_res, dev_starts, dev_ends, req_count, token_rank)

    group_ids, adapter_hot = token_groups(token_rank, request_length, request_group, adapter_per_group)
    shift_rows = jnp.take(modulation[:, 0, :], group_ids, axis=0)
    scale_rows = jnp.take(modulation[:, 1, :], group_ids, axis=0)
    gate_table = lax.dynamic_slice_in_dim(modulation[:, 2, :], column_index * width, width, 1)
    gate_rows = jnp.take(gate_table, group_ids, axis=0)

    head_terms = jnp.einsum(
        "tk,kmc->mtc",
        attention_rows,
        out_w.reshape(head_width, mlp_count, width),
        preferred_element_type=jnp.float32,
    )
    out_low = select_low(
        jnp.dot(
            attention_rows,
            output_down_maps.reshape(head_width, ADAPTER_TOTAL * ADAPTER_RANK),
            preferred_element_type=jnp.float32,
        ),
        adapter_hot,
    )
    low_count = out_low.size
    low_rows = -(-low_count // width)
    low_flat = jnp.pad(out_low.reshape(-1), (0, low_rows * width - low_count)).reshape(
        1, low_rows, width
    )
    send = jnp.concatenate(
        [head_terms, jnp.broadcast_to(low_flat, (mlp_count, low_rows, width))], axis=1
    ).astype(jnp.bfloat16)
    summed = scatter_mlp(send.reshape((Y_COUNT, mlp_count // Y_COUNT) + send.shape[1:]))
    projection_rows = summed[:tok_dev]
    output_rank_values = (
        summed[tok_dev:].reshape(-1)[:low_count].reshape(tok_dev, ADAPTER_RANK).astype(jnp.bfloat16)
    )
    adapter_delta = jnp.dot(
        expand_rank_rows(output_rank_values, adapter_hot),
        output_up_maps.reshape(ADAPTER_TOTAL * ADAPTER_RANK, width),
        preferred_element_type=jnp.float32,
    )
    blended_rows = (residual_rows.astype(jnp.float32) + projection_rows + adapter_delta).astype(
        jnp.bfloat16
    )
    values = blended_rows.astype(jnp.float32)

    full_rows = gather_mlp(blended_rows, Y_COUNT).astype(jnp.float32)
    row_mean = jnp.sum(full_rows, axis=(0, 2)) / MODEL_WIDTH
    variance = jnp.sum(full_rows * full_rows, axis=(0, 2)) / MODEL_WIDTH - row_mean * row_mean
    inv = lax.rsqrt(variance + norm_epsilon)
    scale_m = (1.0 + scale_rows).reshape(-1, mlp_count, width).transpose(1, 0, 2)
    shift_m = shift_rows.reshape(-1, mlp_count, width).transpose(1, 0, 2)
    normalized = (
        (full_rows - row_mean[None, :, None]) * inv[None, :, None] * scale_m + shift_m
    ).astype(jnp.bfloat16)

    normed_local = lax.dynamic_index_in_dim(normalized, column_index, 0, keepdims=False)
    part_low = jnp.dot(
        normed_local,
        hidden_down_maps.reshape(width, ADAPTER_TOTAL * ADAPTER_RANK),
        preferred_element_type=jnp.float32,
    )
    hidden_rank_values = mlp_sum(select_low(part_low, adapter_hot).astype(jnp.bfloat16)).astype(
        jnp.bfloat16
    )
    hidden_units = up_weight.shape[1]
    hidden_total = jnp.einsum(
        "mtc,mch->th",
        normalized,
        up_w.reshape(mlp_count, width, hidden_units),
        preferred_element_type=jnp.float32,
    )
    hidden_total = hidden_total + jnp.dot(
        expand_rank_rows(hidden_rank_values, adapter_hot),
        hidden_up_maps.reshape(ADAPTER_TOTAL * ADAPTER_RANK, hidden_units),
        preferred_element_type=jnp.float32,
    )
    hidden = jax.nn.gelu(hidden_total, approximate=True).astype(jnp.bfloat16)
    down_terms = jnp.einsum(
        "th,mch->mtc",
        hidden,
        down_t.reshape(mlp_count, width, hidden_units),
        preferred_element_type=jnp.float32,
    ).astype(jnp.bfloat16)
    down_sum = scatter_mlp(
        down_terms.reshape((Y_COUNT, mlp_count // Y_COUNT) + down_terms.shape[1:])
    )
    result = (values + gate_rows * down_sum).astype(jnp.bfloat16)
    return result.reshape(tok_dev, 1, width)


def solution(mesh):
    placed = (
        P("req", "mlp"),
        P("req", "mlp"),
        P(),
        P(),
        P(),
        P("mlp", "req"),
        P("mlp", None, None),
        P(None, None, "mlp"),
        P(),
        P("mlp", None, None),
        P(None, None, "mlp"),
        P("req", "mlp"),
        P("mlp", "req"),
    )
    return jax.shard_map(
        local, mesh=mesh, in_specs=placed, out_specs=P(None, "req", "mlp"), check_vma=False
    )
```

```python
import jax
import jax.numpy as jnp
from jax import lax
from jax.sharding import PartitionSpec as P

MODEL_WIDTH = 5120
ADAPTER_RANK = 16
ADAPTER_TOTAL = 16
TOK_DEV = 384
Y_COUNT = 4


norm_epsilon = 1e-06


def send_layout(packed, offset, req_count):
    shaped = packed.reshape(packed.shape[0] // req_count, req_count, packed.shape[1])
    return jnp.roll(shaped, offset, axis=1)


def compact(moved, starts, ends, req_count, token_rank):
    slots = moved.shape[0] * moved.shape[1]
    flat_rows = moved.reshape(slots, moved.shape[2])
    source = jnp.sum((ends[None, :] <= token_rank[:, None]).astype(jnp.int32), axis=1)
    source_hot = source[:, None] == jnp.arange(req_count, dtype=jnp.int32)[None, :]
    source_start = jnp.sum(jnp.where(source_hot, starts[None, :], 0), axis=1)
    position = (token_rank - source_start) // req_count * req_count + source
    return jnp.take(flat_rows, position, axis=0)


def token_groups(token_rank, request_length, request_group, adapter_per_group):
    req_ends = jnp.cumsum(request_length.reshape(-1))
    request_count = req_ends.shape[0]
    request = jnp.sum((req_ends[None, :] <= token_rank[:, None]).astype(jnp.int32), axis=1)
    request = jnp.minimum(request, request_count - 1)
    request_hot = request[:, None] == jnp.arange(request_count, dtype=jnp.int32)[None, :]
    group_ids = jnp.sum(jnp.where(request_hot, request_group[None, :], 0), axis=1)
    group_count = adapter_per_group.shape[0]
    group_hot = group_ids[:, None] == jnp.arange(group_count, dtype=jnp.int32)[None, :]
    adapter_of_row = jnp.sum(jnp.where(group_hot, adapter_per_group[None, :], 0), axis=1)
    adapter_hot = (
        adapter_of_row[:, None] == jnp.arange(ADAPTER_TOTAL, dtype=jnp.int32)[None, :]
    ).astype(jnp.float32)
    return group_ids, adapter_hot


def select_low(output_rank_rows, adapter_hot):
    shaped = output_rank_rows.reshape(output_rank_rows.shape[0], ADAPTER_TOTAL, ADAPTER_RANK)
    return jnp.sum(shaped * adapter_hot[:, :, None], axis=1)


def expand_rank_rows(low_rows, adapter_hot):
    spread_rows = adapter_hot.astype(jnp.bfloat16)[:, :, None] * low_rows[:, None, :]
    return spread_rows.reshape(low_rows.shape[0], ADAPTER_TOTAL * ADAPTER_RANK)


def mlp_sum(part):
    n = lax.axis_size("mlp")
    total = part.astype(jnp.float32)
    bit = 1
    while bit < n:
        total = total + lax.ppermute(total, "mlp", [(i, i ^ bit) for i in range(n)])
        bit *= 2
    return total


def mlp_move(block, target):
    n = lax.axis_size("mlp")
    return lax.ppermute(block, "mlp", [(i, target(i)) for i in range(n)])


def y_shift(step, y_count):
    return lambda i: ((i // 2 + step) % y_count) * 2 + i % 2


def scatter_mlp(payload):
    y_count = payload.shape[0]
    m = lax.axis_index("mlp")
    y_here = m // 2
    core = m % 2
    mine = lax.dynamic_index_in_dim(payload, core, 1, keepdims=False)
    other = lax.dynamic_index_in_dim(payload, 1 - core, 1, keepdims=False)
    pair = mine.astype(jnp.float32) + mlp_move(other, lambda i: i ^ 1).astype(jnp.float32)

    def chunk(step):
        return lax.dynamic_index_in_dim(pair, (y_here + step) % y_count, 0, keepdims=False)

    far = chunk(2)
    cut = far.shape[0] // 2
    via_right = mlp_move(far[:cut].astype(jnp.bfloat16), y_shift(1, y_count))
    via_left = mlp_move(far[cut:].astype(jnp.bfloat16), y_shift(-1, y_count))
    right = chunk(1)
    right = jnp.concatenate([right[:cut] + via_right.astype(jnp.float32), right[cut:]], axis=0)
    left = chunk(-1)
    left = jnp.concatenate([left[:cut], left[cut:] + via_left.astype(jnp.float32)], axis=0)
    total = chunk(0)
    total = total + mlp_move(right.astype(jnp.bfloat16), y_shift(1, y_count)).astype(jnp.float32)
    total = total + mlp_move(left.astype(jnp.bfloat16), y_shift(-1, y_count)).astype(jnp.float32)
    return total


def gather_mlp(block, y_count):
    m = lax.axis_index("mlp")
    y_here = m // 2
    core = m % 2
    pair = jnp.stack([block, mlp_move(block, lambda i: i ^ 1)], axis=0)
    from_left = mlp_move(pair, y_shift(1, y_count))
    from_right = mlp_move(pair, y_shift(-1, y_count))
    far = jnp.concatenate(
        [mlp_move(from_left[:1], y_shift(1, y_count)), mlp_move(from_right[1:], y_shift(-1, y_count))],
        axis=0,
    )
    held = jnp.stack([pair, from_left, far, from_right], axis=0).reshape((2 * y_count,) + block.shape)
    target = jnp.arange(2 * y_count, dtype=jnp.int32)
    slot = ((y_here - target // 2) % y_count) * 2 + (target % 2) ^ core
    return jnp.take(held, slot, axis=0)


def local(
    residual_input,
    attention_output,
    request_length,
    request_group,
    adapter_per_group,
    output_weight,
    output_down_maps,
    output_up_maps,
    modulation,
    hidden_down_maps,
    hidden_up_maps,
    up_weight,
    down_weight,
):
    req_count = lax.axis_size("req")
    mlp_count = lax.axis_size("mlp")
    device_index = lax.axis_index("req")
    column_index = lax.axis_index("mlp")
    width = residual_input.shape[1]
    head_width = attention_output.shape[1]

    out_w = lax.all_gather(output_weight, "req", axis=1, tiled=True)
    both = jnp.stack([up_weight, down_weight.T], axis=0)
    both = lax.all_gather(both, "req", axis=1, tiled=True)
    up_w = both[0]
    down_t = both[1]

    live_rows = jnp.sum(request_length, axis=1)
    dev_ends = jnp.cumsum(live_rows)
    dev_starts = dev_ends - live_rows
    offset = dev_starts[device_index]
    tok_dev = TOK_DEV
    token_rank = jnp.arange(tok_dev, dtype=jnp.int32) * req_count + device_index
    moved_attn = lax.all_to_all(
        send_layout(attention_output, offset, req_count), "req", split_axis=1, concat_axis=1, tiled=True
    )
    attention_rows = compact(moved_attn, dev_starts, dev_ends, req_count, token_rank)
    moved_res = lax.all_to_all(
        send_layout(residual_input, offset, req_count), "req", split_axis=1, concat_axis=1, tiled=True
    )
    residual_rows = compact(moved_res, dev_starts, dev_ends, req_count, token_rank)

    group_ids, adapter_hot = token_groups(token_rank, request_length, request_group, adapter_per_group)
    shift_rows = jnp.take(modulation[:, 0, :], group_ids, axis=0)
    scale_rows = jnp.take(modulation[:, 1, :], group_ids, axis=0)
    gate_table = lax.dynamic_slice_in_dim(modulation[:, 2, :], column_index * width, width, 1)
    gate_rows = jnp.take(gate_table, group_ids, axis=0)

    head_terms = jnp.einsum(
        "tk,kmc->mtc",
        attention_rows,
        out_w.reshape(head_width, mlp_count, width),
        preferred_element_type=jnp.float32,
    )
    out_low = select_low(
        jnp.dot(
            attention_rows,
            output_down_maps.reshape(head_width, ADAPTER_TOTAL * ADAPTER_RANK),
            preferred_element_type=jnp.float32,
        ),
        adapter_hot,
    )
    low_count = out_low.size
    low_rows = -(-low_count // width)
    low_flat = jnp.pad(out_low.reshape(-1), (0, low_rows * width - low_count)).reshape(
        1, low_rows, width
    )
    send = jnp.concatenate(
        [head_terms, jnp.broadcast_to(low_flat, (mlp_count, low_rows, width))], axis=1
    ).astype(jnp.bfloat16)
    summed = scatter_mlp(send.reshape((Y_COUNT, mlp_count // Y_COUNT) + send.shape[1:]))
    projection_rows = summed[:tok_dev]
    output_rank_values = (
        summed[tok_dev:].reshape(-1)[:low_count].reshape(tok_dev, ADAPTER_RANK).astype(jnp.bfloat16)
    )
    adapter_delta = jnp.dot(
        expand_rank_rows(output_rank_values, adapter_hot),
        output_up_maps.reshape(ADAPTER_TOTAL * ADAPTER_RANK, width),
        preferred_element_type=jnp.float32,
    )
    blended_rows = (residual_rows.astype(jnp.float32) + projection_rows + adapter_delta).astype(
        jnp.bfloat16
    )
    values = blended_rows.astype(jnp.float32)

    full_rows = gather_mlp(blended_rows, Y_COUNT).astype(jnp.float32)
    row_mean = jnp.sum(full_rows, axis=(0, 2)) / MODEL_WIDTH
    variance = jnp.sum(full_rows * full_rows, axis=(0, 2)) / MODEL_WIDTH - row_mean * row_mean
    inv = lax.rsqrt(variance + norm_epsilon)
    scale_m = (1.0 + scale_rows).reshape(-1, mlp_count, width).transpose(1, 0, 2)
    shift_m = shift_rows.reshape(-1, mlp_count, width).transpose(1, 0, 2)
    normalized = (
        (full_rows - row_mean[None, :, None]) * inv[None, :, None] * scale_m + shift_m
    ).astype(jnp.bfloat16)

    normed_local = lax.dynamic_index_in_dim(normalized, column_index, 0, keepdims=False)
    part_low = jnp.dot(
        normed_local,
        hidden_down_maps.reshape(width, ADAPTER_TOTAL * ADAPTER_RANK),
        preferred_element_type=jnp.float32,
    )
    hidden_rank_values = mlp_sum(select_low(part_low, adapter_hot).astype(jnp.bfloat16)).astype(
        jnp.bfloat16
    )
    hidden_units = up_weight.shape[1]
    hidden_total = jnp.einsum(
        "mtc,mch->th",
        normalized,
        up_w.reshape(mlp_count, width, hidden_units),
        preferred_element_type=jnp.float32,
    )
    hidden_total = hidden_total + jnp.dot(
        expand_rank_rows(hidden_rank_values, adapter_hot),
        hidden_up_maps.reshape(ADAPTER_TOTAL * ADAPTER_RANK, hidden_units),
        preferred_element_type=jnp.float32,
    )
    hidden = jax.nn.gelu(hidden_total, approximate=True).astype(jnp.bfloat16)
    down_terms = jnp.einsum(
        "th,mch->mtc",
        hidden,
        down_t.reshape(mlp_count, width, hidden_units),
        preferred_element_type=jnp.float32,
    ).astype(jnp.bfloat16)
    down_sum = scatter_mlp(
        down_terms.reshape((Y_COUNT, mlp_count // Y_COUNT) + down_terms.shape[1:])
    )
    result = (values + gate_rows * down_sum).astype(jnp.bfloat16)
    return result.reshape(tok_dev, 1, width)


def solution(mesh):
    placed = (
        P("req", "mlp"),
        P("req", "mlp"),
        P(),
        P(),
        P(),
        P("mlp", "req"),
        P("mlp", None, None),
        P(None, None, "mlp"),
        P(),
        P("mlp", None, None),
        P(None, None, "mlp"),
        P("req", "mlp"),
        P("mlp", "req"),
    )
    return jax.shard_map(
        local, mesh=mesh, in_specs=placed, out_specs=P(None, "req", "mlp"), check_vma=False
    )
```

```python
import jax
import jax.numpy as jnp
from jax import lax
from jax.sharding import PartitionSpec as P

MODEL_WIDTH = 5120
ADAPTER_RANK = 16
ADAPTER_TOTAL = 16
TOK_DEV = 384
Y_COUNT = 4


norm_epsilon = 1e-06


def send_layout(packed, offset, req_count):
    shaped = packed.reshape(packed.shape[0] // req_count, req_count, packed.shape[1])
    return jnp.roll(shaped, offset, axis=1)


def compact(moved, starts, ends, req_count, token_rank):
    slots = moved.shape[0] * moved.shape[1]
    flat_rows = moved.reshape(slots, moved.shape[2])
    source = jnp.sum((ends[None, :] <= token_rank[:, None]).astype(jnp.int32), axis=1)
    source_hot = source[:, None] == jnp.arange(req_count, dtype=jnp.int32)[None, :]
    source_start = jnp.sum(jnp.where(source_hot, starts[None, :], 0), axis=1)
    position = (token_rank - source_start) // req_count * req_count + source
    return jnp.take(flat_rows, position, axis=0)


def token_groups(token_rank, request_length, request_group, adapter_per_group):
    req_ends = jnp.cumsum(request_length.reshape(-1))
    request_count = req_ends.shape[0]
    request = jnp.sum((req_ends[None, :] <= token_rank[:, None]).astype(jnp.int32), axis=1)
    request = jnp.minimum(request, request_count - 1)
    request_hot = request[:, None] == jnp.arange(request_count, dtype=jnp.int32)[None, :]
    group_ids = jnp.sum(jnp.where(request_hot, request_group[None, :], 0), axis=1)
    group_count = adapter_per_group.shape[0]
    group_hot = group_ids[:, None] == jnp.arange(group_count, dtype=jnp.int32)[None, :]
    adapter_of_row = jnp.sum(jnp.where(group_hot, adapter_per_group[None, :], 0), axis=1)
    adapter_hot = (
        adapter_of_row[:, None] == jnp.arange(ADAPTER_TOTAL, dtype=jnp.int32)[None, :]
    ).astype(jnp.float32)
    return group_ids, adapter_hot


def select_low(output_rank_rows, adapter_hot):
    shaped = output_rank_rows.reshape(output_rank_rows.shape[0], ADAPTER_TOTAL, ADAPTER_RANK)
    return jnp.sum(shaped * adapter_hot[:, :, None], axis=1)


def expand_rank_rows(low_rows, adapter_hot):
    spread_rows = adapter_hot.astype(jnp.bfloat16)[:, :, None] * low_rows[:, None, :]
    return spread_rows.reshape(low_rows.shape[0], ADAPTER_TOTAL * ADAPTER_RANK)


def mlp_sum(part):
    n = lax.axis_size("mlp")
    total = part.astype(jnp.float32)
    bit = 1
    while bit < n:
        total = total + lax.ppermute(total, "mlp", [(i, i ^ bit) for i in range(n)])
        bit *= 2
    return total


def mlp_move(block, target):
    n = lax.axis_size("mlp")
    return lax.ppermute(block, "mlp", [(i, target(i)) for i in range(n)])


def y_shift(step, y_count):
    return lambda i: ((i // 2 + step) % y_count) * 2 + i % 2


def scatter_mlp(payload):
    core = lax.axis_index("mlp") % 2
    mine = lax.dynamic_index_in_dim(payload, core, 1, keepdims=False)
    other = lax.dynamic_index_in_dim(payload, 1 - core, 1, keepdims=False)
    return scatter_pair(mine, other)


def scatter_pair(mine, other):
    y_count = mine.shape[0]
    y_here = lax.axis_index("mlp") // 2
    pair = mine.astype(jnp.float32) + mlp_move(other, lambda i: i ^ 1).astype(jnp.float32)

    def chunk(step):
        return lax.dynamic_index_in_dim(pair, (y_here + step) % y_count, 0, keepdims=False)

    far = chunk(2)
    cut = far.shape[0] // 2
    via_right = mlp_move(far[:cut].astype(jnp.bfloat16), y_shift(1, y_count))
    via_left = mlp_move(far[cut:].astype(jnp.bfloat16), y_shift(-1, y_count))
    right = chunk(1)
    right = jnp.concatenate([right[:cut] + via_right.astype(jnp.float32), right[cut:]], axis=0)
    left = chunk(-1)
    left = jnp.concatenate([left[:cut], left[cut:] + via_left.astype(jnp.float32)], axis=0)
    total = chunk(0)
    total = total + mlp_move(right.astype(jnp.bfloat16), y_shift(1, y_count)).astype(jnp.float32)
    total = total + mlp_move(left.astype(jnp.bfloat16), y_shift(-1, y_count)).astype(jnp.float32)
    return total


def gather_mlp(block, y_count):
    m = lax.axis_index("mlp")
    y_here = m // 2
    core = m % 2
    pair = jnp.stack([block, mlp_move(block, lambda i: i ^ 1)], axis=0)
    from_left = mlp_move(pair, y_shift(1, y_count))
    from_right = mlp_move(pair, y_shift(-1, y_count))
    far = jnp.concatenate(
        [mlp_move(from_left[:1], y_shift(1, y_count)), mlp_move(from_right[1:], y_shift(-1, y_count))],
        axis=0,
    )
    held = jnp.stack([pair, from_left, far, from_right], axis=0).reshape((2 * y_count,) + block.shape)
    target = jnp.arange(2 * y_count, dtype=jnp.int32)
    slot = ((y_here - target // 2) % y_count) * 2 + (target % 2) ^ core
    return jnp.take(held, slot, axis=0)


def local(
    residual_input,
    attention_output,
    request_length,
    request_group,
    adapter_per_group,
    output_weight,
    output_down_maps,
    output_up_maps,
    modulation,
    hidden_down_maps,
    hidden_up_maps,
    up_weight,
    down_weight,
):
    req_count = lax.axis_size("req")
    mlp_count = lax.axis_size("mlp")
    device_index = lax.axis_index("req")
    column_index = lax.axis_index("mlp")
    width = residual_input.shape[1]
    head_width = attention_output.shape[1]

    out_w = lax.all_gather(output_weight, "req", axis=1, tiled=True)
    both = jnp.stack([up_weight, down_weight.T], axis=0)
    both = lax.all_gather(both, "req", axis=1, tiled=True)
    up_w = both[0]
    down_t = both[1]

    live_rows = jnp.sum(request_length, axis=1)
    dev_ends = jnp.cumsum(live_rows)
    dev_starts = dev_ends - live_rows
    offset = dev_starts[device_index]
    tok_dev = TOK_DEV
    token_rank = jnp.arange(tok_dev, dtype=jnp.int32) * req_count + device_index
    moved_attn = lax.all_to_all(
        send_layout(attention_output, offset, req_count), "req", split_axis=1, concat_axis=1, tiled=True
    )
    attention_rows = compact(moved_attn, dev_starts, dev_ends, req_count, token_rank)
    moved_res = lax.all_to_all(
        send_layout(residual_input, offset, req_count), "req", split_axis=1, concat_axis=1, tiled=True
    )
    residual_rows = compact(moved_res, dev_starts, dev_ends, req_count, token_rank)

    group_ids, adapter_hot = token_groups(token_rank, request_length, request_group, adapter_per_group)
    shift_rows = jnp.take(modulation[:, 0, :], group_ids, axis=0)
    scale_rows = jnp.take(modulation[:, 1, :], group_ids, axis=0)
    gate_table = lax.dynamic_slice_in_dim(modulation[:, 2, :], column_index * width, width, 1)
    gate_rows = jnp.take(gate_table, group_ids, axis=0)

    head_terms = jnp.einsum(
        "tk,kmc->mtc",
        attention_rows,
        out_w.reshape(head_width, mlp_count, width),
        preferred_element_type=jnp.float32,
    )
    out_low = select_low(
        jnp.dot(
            attention_rows,
            output_down_maps.reshape(head_width, ADAPTER_TOTAL * ADAPTER_RANK),
            preferred_element_type=jnp.float32,
        ),
        adapter_hot,
    )
    low_count = out_low.size
    low_rows = -(-low_count // width)
    low_flat = jnp.pad(out_low.reshape(-1), (0, low_rows * width - low_count)).reshape(
        1, low_rows, width
    )
    send = jnp.concatenate(
        [head_terms, jnp.broadcast_to(low_flat, (mlp_count, low_rows, width))], axis=1
    ).astype(jnp.bfloat16)
    summed = scatter_mlp(send.reshape((Y_COUNT, mlp_count // Y_COUNT) + send.shape[1:]))
    projection_rows = summed[:tok_dev]
    output_rank_values = (
        summed[tok_dev:].reshape(-1)[:low_count].reshape(tok_dev, ADAPTER_RANK).astype(jnp.bfloat16)
    )
    adapter_delta = jnp.dot(
        expand_rank_rows(output_rank_values, adapter_hot),
        output_up_maps.reshape(ADAPTER_TOTAL * ADAPTER_RANK, width),
        preferred_element_type=jnp.float32,
    )
    blended_rows = (residual_rows.astype(jnp.float32) + projection_rows + adapter_delta).astype(
        jnp.bfloat16
    )
    values = blended_rows.astype(jnp.float32)

    full_rows = gather_mlp(blended_rows, Y_COUNT).astype(jnp.float32)
    row_mean = jnp.sum(full_rows, axis=(0, 2)) / MODEL_WIDTH
    variance = jnp.sum(full_rows * full_rows, axis=(0, 2)) / MODEL_WIDTH - row_mean * row_mean
    inv = lax.rsqrt(variance + norm_epsilon)
    scale_m = (1.0 + scale_rows).reshape(-1, mlp_count, width).transpose(1, 0, 2)
    shift_m = shift_rows.reshape(-1, mlp_count, width).transpose(1, 0, 2)
    normalized = (
        (full_rows - row_mean[None, :, None]) * inv[None, :, None] * scale_m + shift_m
    ).astype(jnp.bfloat16)

    normed_local = lax.dynamic_index_in_dim(normalized, column_index, 0, keepdims=False)
    part_low = jnp.dot(
        normed_local,
        hidden_down_maps.reshape(width, ADAPTER_TOTAL * ADAPTER_RANK),
        preferred_element_type=jnp.float32,
    )
    hidden_rank_values = mlp_sum(select_low(part_low, adapter_hot).astype(jnp.bfloat16)).astype(
        jnp.bfloat16
    )
    hidden_units = up_weight.shape[1]
    hidden_total = jnp.einsum(
        "mtc,mch->th",
        normalized,
        up_w.reshape(mlp_count, width, hidden_units),
        preferred_element_type=jnp.float32,
    )
    hidden_total = hidden_total + jnp.dot(
        expand_rank_rows(hidden_rank_values, adapter_hot),
        hidden_up_maps.reshape(ADAPTER_TOTAL * ADAPTER_RANK, hidden_units),
        preferred_element_type=jnp.float32,
    )
    hidden = jax.nn.gelu(hidden_total, approximate=True).astype(jnp.bfloat16)
    core = column_index % 2
    down_by_core = down_t.reshape(Y_COUNT, mlp_count // Y_COUNT, width, hidden_units)
    down_parts = [
        jnp.einsum(
            "th,ych->ytc",
            hidden,
            lax.dynamic_index_in_dim(down_by_core, pick, 1, keepdims=False),
            preferred_element_type=jnp.float32,
        ).astype(jnp.bfloat16)
        for pick in (1 - core, core)
    ]
    down_sum = scatter_pair(lax.optimization_barrier(down_parts[1]), down_parts[0])
    result = (values + gate_rows * down_sum).astype(jnp.bfloat16)
    return result.reshape(tok_dev, 1, width)


def solution(mesh):
    placed = (
        P("req", "mlp"),
        P("req", "mlp"),
        P(),
        P(),
        P(),
        P("mlp", "req"),
        P("mlp", None, None),
        P(None, None, "mlp"),
        P(),
        P("mlp", None, None),
        P(None, None, "mlp"),
        P("req", "mlp"),
        P("mlp", "req"),
    )
    return jax.shard_map(
        local, mesh=mesh, in_specs=placed, out_specs=P(None, "req", "mlp"), check_vma=False
    )
```

```python
import jax
import jax.numpy as jnp
from jax import lax
from jax.sharding import PartitionSpec as P

MODEL_WIDTH = 5120
ADAPTER_RANK = 16
ADAPTER_TOTAL = 16
TOK_DEV = 384
Y_COUNT = 4
Z_COUNT = 4


norm_epsilon = 1e-06


def send_layout(packed, offset, req_count):
    shaped = packed.reshape(packed.shape[0] // req_count, req_count, packed.shape[1])
    return jnp.roll(shaped, offset, axis=1)


def compact(moved, starts, ends, req_count, token_rank):
    slots = moved.shape[0] * moved.shape[1]
    flat_rows = moved.reshape(slots, moved.shape[2])
    source = jnp.sum((ends[None, :] <= token_rank[:, None]).astype(jnp.int32), axis=1)
    source_hot = source[:, None] == jnp.arange(req_count, dtype=jnp.int32)[None, :]
    source_start = jnp.sum(jnp.where(source_hot, starts[None, :], 0), axis=1)
    position = (token_rank - source_start) // req_count * req_count + source
    return jnp.take(flat_rows, position, axis=0)


def token_groups(token_rank, request_length, request_group, adapter_per_group):
    req_ends = jnp.cumsum(request_length.reshape(-1))
    request_count = req_ends.shape[0]
    request = jnp.sum((req_ends[None, :] <= token_rank[:, None]).astype(jnp.int32), axis=1)
    request = jnp.minimum(request, request_count - 1)
    request_hot = request[:, None] == jnp.arange(request_count, dtype=jnp.int32)[None, :]
    group_ids = jnp.sum(jnp.where(request_hot, request_group[None, :], 0), axis=1)
    group_count = adapter_per_group.shape[0]
    group_hot = group_ids[:, None] == jnp.arange(group_count, dtype=jnp.int32)[None, :]
    adapter_of_row = jnp.sum(jnp.where(group_hot, adapter_per_group[None, :], 0), axis=1)
    adapter_hot = (
        adapter_of_row[:, None] == jnp.arange(ADAPTER_TOTAL, dtype=jnp.int32)[None, :]
    ).astype(jnp.float32)
    return group_ids, adapter_hot


def select_low(output_rank_rows, adapter_hot):
    shaped = output_rank_rows.reshape(output_rank_rows.shape[0], ADAPTER_TOTAL, ADAPTER_RANK)
    return jnp.sum(shaped * adapter_hot[:, :, None], axis=1)


def expand_rank_rows(low_rows, adapter_hot):
    spread_rows = adapter_hot.astype(jnp.bfloat16)[:, :, None] * low_rows[:, None, :]
    return spread_rows.reshape(low_rows.shape[0], ADAPTER_TOTAL * ADAPTER_RANK)


def mlp_sum(part):
    n = lax.axis_size("mlp")
    total = part.astype(jnp.float32)
    bit = 1
    while bit < n:
        total = total + lax.ppermute(total, "mlp", [(i, i ^ bit) for i in range(n)])
        bit *= 2
    return total


def mlp_move(block, target):
    n = lax.axis_size("mlp")
    return lax.ppermute(block, "mlp", [(i, target(i)) for i in range(n)])


def y_shift(step, y_count):
    return lambda i: ((i // 2 + step) % y_count) * 2 + i % 2


def scatter_mlp(payload):
    core = lax.axis_index("mlp") % 2
    mine = lax.dynamic_index_in_dim(payload, core, 1, keepdims=False)
    other = lax.dynamic_index_in_dim(payload, 1 - core, 1, keepdims=False)
    return scatter_pair(mine, other)


def scatter_pair(mine, other):
    y_count = mine.shape[0]
    y_here = lax.axis_index("mlp") // 2
    pair = mine.astype(jnp.float32) + mlp_move(other, lambda i: i ^ 1).astype(jnp.float32)

    def chunk(step):
        return lax.dynamic_index_in_dim(pair, (y_here + step) % y_count, 0, keepdims=False)

    far = chunk(2)
    cut = far.shape[0] // 2
    via_right = mlp_move(far[:cut].astype(jnp.bfloat16), y_shift(1, y_count))
    via_left = mlp_move(far[cut:].astype(jnp.bfloat16), y_shift(-1, y_count))
    right = chunk(1)
    right = jnp.concatenate([right[:cut] + via_right.astype(jnp.float32), right[cut:]], axis=0)
    left = chunk(-1)
    left = jnp.concatenate([left[:cut], left[cut:] + via_left.astype(jnp.float32)], axis=0)
    total = chunk(0)
    total = total + mlp_move(right.astype(jnp.bfloat16), y_shift(1, y_count)).astype(jnp.float32)
    total = total + mlp_move(left.astype(jnp.bfloat16), y_shift(-1, y_count)).astype(jnp.float32)
    return total


def gather_mlp(block, y_count):
    m = lax.axis_index("mlp")
    y_here = m // 2
    core = m % 2
    pair = jnp.stack([block, mlp_move(block, lambda i: i ^ 1)], axis=0)
    from_left = mlp_move(pair, y_shift(1, y_count))
    from_right = mlp_move(pair, y_shift(-1, y_count))
    far = jnp.concatenate(
        [mlp_move(from_left[:1], y_shift(1, y_count)), mlp_move(from_right[1:], y_shift(-1, y_count))],
        axis=0,
    )
    held = jnp.stack([pair, from_left, far, from_right], axis=0).reshape((2 * y_count,) + block.shape)
    target = jnp.arange(2 * y_count, dtype=jnp.int32)
    slot = ((y_here - target // 2) % y_count) * 2 + (target % 2) ^ core
    return jnp.take(held, slot, axis=0)


def req_shift(block, z_count, x_count, along, step):
    pairs = []
    for z in range(z_count):
        for x in range(x_count):
            if along == "x":
                pairs.append((z * x_count + x, z * x_count + (x + step) % x_count))
            else:
                pairs.append((z * x_count + x, ((z + step) % z_count) * x_count + x))
    return lax.ppermute(block, "req", pairs)


def ring_row(stack, z_count, x_count, along):
    from_left = req_shift(stack, z_count, x_count, along, 1)
    from_right = req_shift(stack, z_count, x_count, along, -1)
    n = stack.shape[0]
    if n >= 2:
        far = jnp.concatenate(
            [
                req_shift(from_left[: n // 2], z_count, x_count, along, 1),
                req_shift(from_right[n // 2 :], z_count, x_count, along, -1),
            ],
            axis=0,
        )
    else:
        cut = stack.shape[1] // 2
        far = jnp.concatenate(
            [
                req_shift(from_left[:, :cut], z_count, x_count, along, 1),
                req_shift(from_right[:, cut:], z_count, x_count, along, -1),
            ],
            axis=1,
        )
    return jnp.stack([stack, from_right, far, from_left], axis=0)


def ring_gather_req(block, z_count, x_count):
    row = ring_row(block[None], z_count, x_count, "x")[:, 0]
    held = ring_row(row, z_count, x_count, "z").reshape((z_count * x_count,) + block.shape)
    r = lax.axis_index("req")
    target = jnp.arange(z_count * x_count, dtype=jnp.int32)
    rel = ((target // x_count - r // x_count) % z_count) * x_count + (target % x_count - r % x_count) % x_count
    return jnp.take(held, rel, axis=0)


def local(
    residual_input,
    attention_output,
    request_length,
    request_group,
    adapter_per_group,
    output_weight,
    output_down_maps,
    output_up_maps,
    modulation,
    hidden_down_maps,
    hidden_up_maps,
    up_weight,
    down_weight,
):
    req_count = lax.axis_size("req")
    mlp_count = lax.axis_size("mlp")
    device_index = lax.axis_index("req")
    column_index = lax.axis_index("mlp")
    width = residual_input.shape[1]
    head_width = attention_output.shape[1]

    out_w = ring_gather_req(output_weight, Z_COUNT, req_count // Z_COUNT)
    out_w = out_w.transpose(1, 0, 2).reshape(output_weight.shape[0], -1)
    both = jnp.stack([up_weight, down_weight.T], axis=0)
    both = lax.all_gather(both, "req", axis=1, tiled=True)
    up_w = both[0]
    down_t = both[1]

    live_rows = jnp.sum(request_length, axis=1)
    dev_ends = jnp.cumsum(live_rows)
    dev_starts = dev_ends - live_rows
    offset = dev_starts[device_index]
    tok_dev = TOK_DEV
    token_rank = jnp.arange(tok_dev, dtype=jnp.int32) * req_count + device_index
    moved_attn = lax.all_to_all(
        send_layout(attention_output, offset, req_count), "req", split_axis=1, concat_axis=1, tiled=True
    )
    attention_rows = compact(moved_attn, dev_starts, dev_ends, req_count, token_rank)
    moved_res = lax.all_to_all(
        send_layout(residual_input, offset, req_count), "req", split_axis=1, concat_axis=1, tiled=True
    )
    residual_rows = compact(moved_res, dev_starts, dev_ends, req_count, token_rank)

    group_ids, adapter_hot = token_groups(token_rank, request_length, request_group, adapter_per_group)
    shift_rows = jnp.take(modulation[:, 0, :], group_ids, axis=0)
    scale_rows = jnp.take(modulation[:, 1, :], group_ids, axis=0)
    gate_table = lax.dynamic_slice_in_dim(modulation[:, 2, :], column_index * width, width, 1)
    gate_rows = jnp.take(gate_table, group_ids, axis=0)

    head_terms = jnp.einsum(
        "tk,kmc->mtc",
        attention_rows,
        out_w.reshape(head_width, mlp_count, width),
        preferred_element_type=jnp.float32,
    )
    out_low = select_low(
        jnp.dot(
            attention_rows,
            output_down_maps.reshape(head_width, ADAPTER_TOTAL * ADAPTER_RANK),
            preferred_element_type=jnp.float32,
        ),
        adapter_hot,
    )
    low_count = out_low.size
    low_rows = -(-low_count // width)
    low_flat = jnp.pad(out_low.reshape(-1), (0, low_rows * width - low_count)).reshape(
        1, low_rows, width
    )
    send = jnp.concatenate(
        [head_terms, jnp.broadcast_to(low_flat, (mlp_count, low_rows, width))], axis=1
    ).astype(jnp.bfloat16)
    summed = scatter_mlp(send.reshape((Y_COUNT, mlp_count // Y_COUNT) + send.shape[1:]))
    projection_rows = summed[:tok_dev]
    output_rank_values = (
        summed[tok_dev:].reshape(-1)[:low_count].reshape(tok_dev, ADAPTER_RANK).astype(jnp.bfloat16)
    )
    adapter_delta = jnp.dot(
        expand_rank_rows(output_rank_values, adapter_hot),
        output_up_maps.reshape(ADAPTER_TOTAL * ADAPTER_RANK, width),
        preferred_element_type=jnp.float32,
    )
    blended_rows = (residual_rows.astype(jnp.float32) + projection_rows + adapter_delta).astype(
        jnp.bfloat16
    )
    values = blended_rows.astype(jnp.float32)

    full_rows = gather_mlp(blended_rows, Y_COUNT).astype(jnp.float32)
    row_mean = jnp.sum(full_rows, axis=(0, 2)) / MODEL_WIDTH
    variance = jnp.sum(full_rows * full_rows, axis=(0, 2)) / MODEL_WIDTH - row_mean * row_mean
    inv = lax.rsqrt(variance + norm_epsilon)
    scale_m = (1.0 + scale_rows).reshape(-1, mlp_count, width).transpose(1, 0, 2)
    shift_m = shift_rows.reshape(-1, mlp_count, width).transpose(1, 0, 2)
    normalized = (
        (full_rows - row_mean[None, :, None]) * inv[None, :, None] * scale_m + shift_m
    ).astype(jnp.bfloat16)

    normed_local = lax.dynamic_index_in_dim(normalized, column_index, 0, keepdims=False)
    part_low = jnp.dot(
        normed_local,
        hidden_down_maps.reshape(width, ADAPTER_TOTAL * ADAPTER_RANK),
        preferred_element_type=jnp.float32,
    )
    hidden_rank_values = mlp_sum(select_low(part_low, adapter_hot).astype(jnp.bfloat16)).astype(
        jnp.bfloat16
    )
    hidden_units = up_weight.shape[1]
    hidden_total = jnp.einsum(
        "mtc,mch->th",
        normalized,
        up_w.reshape(mlp_count, width, hidden_units),
        preferred_element_type=jnp.float32,
    )
    hidden_total = hidden_total + jnp.dot(
        expand_rank_rows(hidden_rank_values, adapter_hot),
        hidden_up_maps.reshape(ADAPTER_TOTAL * ADAPTER_RANK, hidden_units),
        preferred_element_type=jnp.float32,
    )
    hidden = jax.nn.gelu(hidden_total, approximate=True).astype(jnp.bfloat16)
    core = column_index % 2
    down_by_core = down_t.reshape(Y_COUNT, mlp_count // Y_COUNT, width, hidden_units)
    down_parts = [
        jnp.einsum(
            "th,ych->ytc",
            hidden,
            lax.dynamic_index_in_dim(down_by_core, pick, 1, keepdims=False),
            preferred_element_type=jnp.float32,
        ).astype(jnp.bfloat16)
        for pick in (1 - core, core)
    ]
    down_sum = scatter_pair(lax.optimization_barrier(down_parts[1]), down_parts[0])
    result = (values + gate_rows * down_sum).astype(jnp.bfloat16)
    return result.reshape(tok_dev, 1, width)


def solution(mesh):
    placed = (
        P("req", "mlp"),
        P("req", "mlp"),
        P(),
        P(),
        P(),
        P("mlp", "req"),
        P("mlp", None, None),
        P(None, None, "mlp"),
        P(),
        P("mlp", None, None),
        P(None, None, "mlp"),
        P("req", "mlp"),
        P("mlp", "req"),
    )
    return jax.shard_map(
        local, mesh=mesh, in_specs=placed, out_specs=P(None, "req", "mlp"), check_vma=False
    )
```

```python
import jax
import jax.numpy as jnp
from jax import lax
from jax.sharding import PartitionSpec as P

MODEL_WIDTH = 5120
ADAPTER_RANK = 16
ADAPTER_TOTAL = 16
TOK_DEV = 384
Y_COUNT = 4


norm_epsilon = 1e-06


def send_layout(packed, offset, req_count):
    shaped = packed.reshape(packed.shape[0] // req_count, req_count, packed.shape[1])
    return jnp.roll(shaped, offset, axis=1)


def compact(moved, starts, ends, req_count, token_rank):
    slots = moved.shape[0] * moved.shape[1]
    flat_rows = moved.reshape(slots, moved.shape[2])
    source = jnp.sum((ends[None, :] <= token_rank[:, None]).astype(jnp.int32), axis=1)
    source_hot = source[:, None] == jnp.arange(req_count, dtype=jnp.int32)[None, :]
    source_start = jnp.sum(jnp.where(source_hot, starts[None, :], 0), axis=1)
    position = (token_rank - source_start) // req_count * req_count + source
    return jnp.take(flat_rows, position, axis=0)


def token_groups(token_rank, request_length, request_group, adapter_per_group):
    req_ends = jnp.cumsum(request_length.reshape(-1))
    request_count = req_ends.shape[0]
    request = jnp.sum((req_ends[None, :] <= token_rank[:, None]).astype(jnp.int32), axis=1)
    request = jnp.minimum(request, request_count - 1)
    request_hot = request[:, None] == jnp.arange(request_count, dtype=jnp.int32)[None, :]
    group_ids = jnp.sum(jnp.where(request_hot, request_group[None, :], 0), axis=1)
    group_count = adapter_per_group.shape[0]
    group_hot = group_ids[:, None] == jnp.arange(group_count, dtype=jnp.int32)[None, :]
    adapter_of_row = jnp.sum(jnp.where(group_hot, adapter_per_group[None, :], 0), axis=1)
    adapter_hot = (
        adapter_of_row[:, None] == jnp.arange(ADAPTER_TOTAL, dtype=jnp.int32)[None, :]
    ).astype(jnp.float32)
    return group_ids, adapter_hot


def select_low(output_rank_rows, adapter_hot):
    shaped = output_rank_rows.reshape(output_rank_rows.shape[0], ADAPTER_TOTAL, ADAPTER_RANK)
    return jnp.sum(shaped * adapter_hot[:, :, None], axis=1)


def expand_rank_rows(low_rows, adapter_hot):
    spread_rows = adapter_hot.astype(jnp.bfloat16)[:, :, None] * low_rows[:, None, :]
    return spread_rows.reshape(low_rows.shape[0], ADAPTER_TOTAL * ADAPTER_RANK)


def mlp_sum(part):
    n = lax.axis_size("mlp")
    total = part.astype(jnp.float32)
    bit = 1
    while bit < n:
        total = total + lax.ppermute(total, "mlp", [(i, i ^ bit) for i in range(n)])
        bit *= 2
    return total


def mlp_move(block, target):
    n = lax.axis_size("mlp")
    return lax.ppermute(block, "mlp", [(i, target(i)) for i in range(n)])


def y_shift(step, y_count):
    return lambda i: ((i // 2 + step) % y_count) * 2 + i % 2


def scatter_mlp(payload):
    core = lax.axis_index("mlp") % 2
    mine = lax.dynamic_index_in_dim(payload, core, 1, keepdims=False)
    other = lax.dynamic_index_in_dim(payload, 1 - core, 1, keepdims=False)
    return scatter_pair(mine, other)


def scatter_pair(mine, other):
    y_count = mine.shape[0]
    y_here = lax.axis_index("mlp") // 2
    pair = mine.astype(jnp.float32) + mlp_move(other, lambda i: i ^ 1).astype(jnp.float32)

    def chunk(step):
        return lax.dynamic_index_in_dim(pair, (y_here + step) % y_count, 0, keepdims=False)

    far = chunk(2)
    cut = far.shape[0] // 2
    via_right = mlp_move(far[:cut].astype(jnp.bfloat16), y_shift(1, y_count))
    via_left = mlp_move(far[cut:].astype(jnp.bfloat16), y_shift(-1, y_count))
    right = chunk(1)
    right = jnp.concatenate([right[:cut] + via_right.astype(jnp.float32), right[cut:]], axis=0)
    left = chunk(-1)
    left = jnp.concatenate([left[:cut], left[cut:] + via_left.astype(jnp.float32)], axis=0)
    total = chunk(0)
    total = total + mlp_move(right.astype(jnp.bfloat16), y_shift(1, y_count)).astype(jnp.float32)
    total = total + mlp_move(left.astype(jnp.bfloat16), y_shift(-1, y_count)).astype(jnp.float32)
    return total


def gather_mlp(block, y_count):
    m = lax.axis_index("mlp")
    y_here = m // 2
    core = m % 2
    pair = jnp.stack([block, mlp_move(block, lambda i: i ^ 1)], axis=0)
    from_left = mlp_move(pair, y_shift(1, y_count))
    from_right = mlp_move(pair, y_shift(-1, y_count))
    far = jnp.concatenate(
        [mlp_move(from_left[:1], y_shift(1, y_count)), mlp_move(from_right[1:], y_shift(-1, y_count))],
        axis=0,
    )
    held = jnp.stack([pair, from_left, far, from_right], axis=0).reshape((2 * y_count,) + block.shape)
    target = jnp.arange(2 * y_count, dtype=jnp.int32)
    slot = ((y_here - target // 2) % y_count) * 2 + (target % 2) ^ core
    return jnp.take(held, slot, axis=0)


def local(
    residual_input,
    attention_output,
    request_length,
    request_group,
    adapter_per_group,
    output_weight,
    output_down_maps,
    output_up_maps,
    modulation,
    hidden_down_maps,
    hidden_up_maps,
    up_weight,
    down_weight,
):
    req_count = lax.axis_size("req")
    mlp_count = lax.axis_size("mlp")
    device_index = lax.axis_index("req")
    column_index = lax.axis_index("mlp")
    width = residual_input.shape[1]
    head_width = attention_output.shape[1]

    out_w = lax.all_gather(output_weight, "req", axis=1, tiled=True)
    both = jnp.stack([up_weight, down_weight.T], axis=0)
    both = lax.all_gather(both, "req", axis=1, tiled=True)
    up_w = both[0]
    down_t = both[1]

    live_rows = jnp.sum(request_length, axis=1)
    dev_ends = jnp.cumsum(live_rows)
    dev_starts = dev_ends - live_rows
    offset = dev_starts[device_index]
    tok_dev = TOK_DEV
    token_rank = jnp.arange(tok_dev, dtype=jnp.int32) * req_count + device_index
    moved_attn = lax.all_to_all(
        send_layout(attention_output, offset, req_count), "req", split_axis=1, concat_axis=1, tiled=True
    )
    moved_res = lax.all_to_all(
        send_layout(residual_input, offset, req_count), "req", split_axis=1, concat_axis=1, tiled=True
    )
    moved_attn, moved_res = lax.optimization_barrier((moved_attn, moved_res))
    attention_rows = compact(moved_attn, dev_starts, dev_ends, req_count, token_rank)
    residual_rows = compact(moved_res, dev_starts, dev_ends, req_count, token_rank)

    group_ids, adapter_hot = token_groups(token_rank, request_length, request_group, adapter_per_group)
    shift_rows = jnp.take(modulation[:, 0, :], group_ids, axis=0)
    scale_rows = jnp.take(modulation[:, 1, :], group_ids, axis=0)
    gate_table = lax.dynamic_slice_in_dim(modulation[:, 2, :], column_index * width, width, 1)
    gate_rows = jnp.take(gate_table, group_ids, axis=0)

    head_terms = jnp.einsum(
        "tk,kmc->mtc",
        attention_rows,
        out_w.reshape(head_width, mlp_count, width),
        preferred_element_type=jnp.float32,
    )
    out_low = select_low(
        jnp.dot(
            attention_rows,
            output_down_maps.reshape(head_width, ADAPTER_TOTAL * ADAPTER_RANK),
            preferred_element_type=jnp.float32,
        ),
        adapter_hot,
    )
    low_count = out_low.size
    low_rows = -(-low_count // width)
    low_flat = jnp.pad(out_low.reshape(-1), (0, low_rows * width - low_count)).reshape(
        1, low_rows, width
    )
    send = jnp.concatenate(
        [head_terms, jnp.broadcast_to(low_flat, (mlp_count, low_rows, width))], axis=1
    ).astype(jnp.bfloat16)
    summed = scatter_mlp(send.reshape((Y_COUNT, mlp_count // Y_COUNT) + send.shape[1:]))
    projection_rows = summed[:tok_dev]
    output_rank_values = (
        summed[tok_dev:].reshape(-1)[:low_count].reshape(tok_dev, ADAPTER_RANK).astype(jnp.bfloat16)
    )
    adapter_delta = jnp.dot(
        expand_rank_rows(output_rank_values, adapter_hot),
        output_up_maps.reshape(ADAPTER_TOTAL * ADAPTER_RANK, width),
        preferred_element_type=jnp.float32,
    )
    blended_rows = (residual_rows.astype(jnp.float32) + projection_rows + adapter_delta).astype(
        jnp.bfloat16
    )
    values = blended_rows.astype(jnp.float32)

    full_rows = gather_mlp(blended_rows, Y_COUNT).astype(jnp.float32)
    row_mean = jnp.sum(full_rows, axis=(0, 2)) / MODEL_WIDTH
    variance = jnp.sum(full_rows * full_rows, axis=(0, 2)) / MODEL_WIDTH - row_mean * row_mean
    inv = lax.rsqrt(variance + norm_epsilon)
    scale_m = (1.0 + scale_rows).reshape(-1, mlp_count, width).transpose(1, 0, 2)
    shift_m = shift_rows.reshape(-1, mlp_count, width).transpose(1, 0, 2)
    normalized = (
        (full_rows - row_mean[None, :, None]) * inv[None, :, None] * scale_m + shift_m
    ).astype(jnp.bfloat16)

    normed_local = lax.dynamic_index_in_dim(normalized, column_index, 0, keepdims=False)
    part_low = jnp.dot(
        normed_local,
        hidden_down_maps.reshape(width, ADAPTER_TOTAL * ADAPTER_RANK),
        preferred_element_type=jnp.float32,
    )
    hidden_rank_values = mlp_sum(select_low(part_low, adapter_hot).astype(jnp.bfloat16)).astype(
        jnp.bfloat16
    )
    hidden_units = up_weight.shape[1]
    hidden_total = jnp.einsum(
        "mtc,mch->th",
        normalized,
        up_w.reshape(mlp_count, width, hidden_units),
        preferred_element_type=jnp.float32,
    )
    hidden_total = hidden_total + jnp.dot(
        expand_rank_rows(hidden_rank_values, adapter_hot),
        hidden_up_maps.reshape(ADAPTER_TOTAL * ADAPTER_RANK, hidden_units),
        preferred_element_type=jnp.float32,
    )
    hidden = jax.nn.gelu(hidden_total, approximate=True).astype(jnp.bfloat16)
    core = column_index % 2
    down_by_core = down_t.reshape(Y_COUNT, mlp_count // Y_COUNT, width, hidden_units)
    down_parts = [
        jnp.einsum(
            "th,ych->ytc",
            hidden,
            lax.dynamic_index_in_dim(down_by_core, pick, 1, keepdims=False),
            preferred_element_type=jnp.float32,
        ).astype(jnp.bfloat16)
        for pick in (1 - core, core)
    ]
    down_sum = scatter_pair(lax.optimization_barrier(down_parts[1]), down_parts[0])
    result = (values + gate_rows * down_sum).astype(jnp.bfloat16)
    return result.reshape(tok_dev, 1, width)


def solution(mesh):
    placed = (
        P("req", "mlp"),
        P("req", "mlp"),
        P(),
        P(),
        P(),
        P("mlp", "req"),
        P("mlp", None, None),
        P(None, None, "mlp"),
        P(),
        P("mlp", None, None),
        P(None, None, "mlp"),
        P("req", "mlp"),
        P("mlp", "req"),
    )
    return jax.shard_map(
        local, mesh=mesh, in_specs=placed, out_specs=P(None, "req", "mlp"), check_vma=False
    )
```

```python
import jax
import jax.numpy as jnp
from jax import lax
from jax.sharding import PartitionSpec as P

MODEL_WIDTH = 5120
ADAPTER_RANK = 16
ADAPTER_TOTAL = 16
TOK_DEV = 384
Y_COUNT = 4


norm_epsilon = 1e-06


def send_layout(packed, offset, req_count):
    shaped = packed.reshape(packed.shape[0] // req_count, req_count, packed.shape[1])
    return jnp.roll(shaped, offset, axis=1)


def compact(moved, starts, ends, req_count, token_rank):
    slots = moved.shape[0] * moved.shape[1]
    flat_rows = moved.reshape(slots, moved.shape[2])
    source = jnp.sum((ends[None, :] <= token_rank[:, None]).astype(jnp.int32), axis=1)
    source_hot = source[:, None] == jnp.arange(req_count, dtype=jnp.int32)[None, :]
    source_start = jnp.sum(jnp.where(source_hot, starts[None, :], 0), axis=1)
    position = (token_rank - source_start) // req_count * req_count + source
    return jnp.take(flat_rows, position, axis=0)


def token_groups(token_rank, request_length, request_group, adapter_per_group):
    req_ends = jnp.cumsum(request_length.reshape(-1))
    request_count = req_ends.shape[0]
    request = jnp.sum((req_ends[None, :] <= token_rank[:, None]).astype(jnp.int32), axis=1)
    request = jnp.minimum(request, request_count - 1)
    request_hot = request[:, None] == jnp.arange(request_count, dtype=jnp.int32)[None, :]
    group_ids = jnp.sum(jnp.where(request_hot, request_group[None, :], 0), axis=1)
    group_count = adapter_per_group.shape[0]
    group_hot = group_ids[:, None] == jnp.arange(group_count, dtype=jnp.int32)[None, :]
    adapter_of_row = jnp.sum(jnp.where(group_hot, adapter_per_group[None, :], 0), axis=1)
    adapter_hot = (
        adapter_of_row[:, None] == jnp.arange(ADAPTER_TOTAL, dtype=jnp.int32)[None, :]
    ).astype(jnp.float32)
    return group_ids, adapter_hot


def select_low(output_rank_rows, adapter_hot):
    shaped = output_rank_rows.reshape(output_rank_rows.shape[0], ADAPTER_TOTAL, ADAPTER_RANK)
    return jnp.sum(shaped * adapter_hot[:, :, None], axis=1)


def expand_rank_rows(low_rows, adapter_hot):
    spread_rows = adapter_hot.astype(jnp.bfloat16)[:, :, None] * low_rows[:, None, :]
    return spread_rows.reshape(low_rows.shape[0], ADAPTER_TOTAL * ADAPTER_RANK)


def mlp_sum(part):
    n = lax.axis_size("mlp")
    total = part.astype(jnp.float32)
    bit = 1
    while bit < n:
        total = total + lax.ppermute(total, "mlp", [(i, i ^ bit) for i in range(n)])
        bit *= 2
    return total


def mlp_move(block, target):
    n = lax.axis_size("mlp")
    return lax.ppermute(block, "mlp", [(i, target(i)) for i in range(n)])


def y_shift(step, y_count):
    return lambda i: ((i // 2 + step) % y_count) * 2 + i % 2


def scatter_mlp(payload):
    core = lax.axis_index("mlp") % 2
    mine = lax.dynamic_index_in_dim(payload, core, 1, keepdims=False)
    other = lax.dynamic_index_in_dim(payload, 1 - core, 1, keepdims=False)
    return scatter_pair(mine, other)


def scatter_pair(mine, other):
    y_count = mine.shape[0]
    y_here = lax.axis_index("mlp") // 2
    pair = mine.astype(jnp.float32) + mlp_move(other, lambda i: i ^ 1).astype(jnp.float32)

    def chunk(step):
        return lax.dynamic_index_in_dim(pair, (y_here + step) % y_count, 0, keepdims=False)

    far = chunk(2)
    cut = far.shape[0] // 2
    via_right = mlp_move(far[:cut].astype(jnp.bfloat16), y_shift(1, y_count))
    via_left = mlp_move(far[cut:].astype(jnp.bfloat16), y_shift(-1, y_count))
    right = chunk(1)
    right = jnp.concatenate([right[:cut] + via_right.astype(jnp.float32), right[cut:]], axis=0)
    left = chunk(-1)
    left = jnp.concatenate([left[:cut], left[cut:] + via_left.astype(jnp.float32)], axis=0)
    total = chunk(0)
    total = total + mlp_move(right.astype(jnp.bfloat16), y_shift(1, y_count)).astype(jnp.float32)
    total = total + mlp_move(left.astype(jnp.bfloat16), y_shift(-1, y_count)).astype(jnp.float32)
    return total


def gather_mlp(block, y_count):
    m = lax.axis_index("mlp")
    y_here = m // 2
    core = m % 2
    pair = jnp.stack([block, mlp_move(block, lambda i: i ^ 1)], axis=0)
    from_left = mlp_move(pair, y_shift(1, y_count))
    from_right = mlp_move(pair, y_shift(-1, y_count))
    far = jnp.concatenate(
        [mlp_move(from_left[:1], y_shift(1, y_count)), mlp_move(from_right[1:], y_shift(-1, y_count))],
        axis=0,
    )
    held = jnp.stack([pair, from_left, far, from_right], axis=0).reshape((2 * y_count,) + block.shape)
    target = jnp.arange(2 * y_count, dtype=jnp.int32)
    slot = ((y_here - target // 2) % y_count) * 2 + (target % 2) ^ core
    return jnp.take(held, slot, axis=0)


def local(
    residual_input,
    attention_output,
    request_length,
    request_group,
    adapter_per_group,
    output_weight,
    output_down_maps,
    output_up_maps,
    modulation,
    hidden_down_maps,
    hidden_up_maps,
    up_weight,
    down_weight,
):
    req_count = lax.axis_size("req")
    mlp_count = lax.axis_size("mlp")
    device_index = lax.axis_index("req")
    column_index = lax.axis_index("mlp")
    width = residual_input.shape[1]
    head_width = attention_output.shape[1]

    out_w = lax.all_gather(output_weight, "req", axis=1, tiled=True)
    both = jnp.stack([up_weight, down_weight.T], axis=0)
    both = lax.all_gather(both, "req", axis=1, tiled=True)
    up_w = both[0]
    down_t = both[1]

    live_rows = jnp.sum(request_length, axis=1)
    dev_ends = jnp.cumsum(live_rows)
    dev_starts = dev_ends - live_rows
    offset = dev_starts[device_index]
    tok_dev = TOK_DEV
    token_rank = jnp.arange(tok_dev, dtype=jnp.int32) * req_count + device_index
    moved_attn = lax.all_to_all(
        send_layout(attention_output, offset, req_count), "req", split_axis=1, concat_axis=1, tiled=True
    )
    moved_res = lax.all_to_all(
        send_layout(residual_input, offset, req_count), "req", split_axis=1, concat_axis=1, tiled=True
    )
    moved_attn, moved_res = lax.optimization_barrier((moved_attn, moved_res))
    attention_rows = compact(moved_attn, dev_starts, dev_ends, req_count, token_rank)
    residual_rows = compact(moved_res, dev_starts, dev_ends, req_count, token_rank)

    group_ids, adapter_hot = token_groups(token_rank, request_length, request_group, adapter_per_group)
    shift_rows = jnp.take(modulation[:, 0, :], group_ids, axis=0)
    scale_rows = jnp.take(modulation[:, 1, :], group_ids, axis=0)
    gate_table = lax.dynamic_slice_in_dim(modulation[:, 2, :], column_index * width, width, 1)
    gate_rows = jnp.take(gate_table, group_ids, axis=0)

    head_terms = jnp.einsum(
        "tk,kmc->mtc",
        attention_rows,
        out_w.reshape(head_width, mlp_count, width),
        preferred_element_type=jnp.float32,
    )
    out_low = select_low(
        jnp.dot(
            attention_rows,
            output_down_maps.reshape(head_width, ADAPTER_TOTAL * ADAPTER_RANK),
            preferred_element_type=jnp.float32,
        ),
        adapter_hot,
    )
    low_count = out_low.size
    low_rows = -(-low_count // width)
    low_flat = jnp.pad(out_low.reshape(-1), (0, low_rows * width - low_count)).reshape(
        1, low_rows, width
    )
    send = jnp.concatenate(
        [head_terms, jnp.broadcast_to(low_flat, (mlp_count, low_rows, width))], axis=1
    ).astype(jnp.bfloat16)
    summed = scatter_mlp(send.reshape((Y_COUNT, mlp_count // Y_COUNT) + send.shape[1:]))
    projection_rows = summed[:tok_dev]
    output_rank_values = (
        summed[tok_dev:].reshape(-1)[:low_count].reshape(tok_dev, ADAPTER_RANK).astype(jnp.bfloat16)
    )
    adapter_delta = jnp.dot(
        expand_rank_rows(output_rank_values, adapter_hot),
        output_up_maps.reshape(ADAPTER_TOTAL * ADAPTER_RANK, width),
        preferred_element_type=jnp.float32,
    )
    blended_rows = (residual_rows.astype(jnp.float32) + projection_rows + adapter_delta).astype(
        jnp.bfloat16
    )
    values = blended_rows.astype(jnp.float32)

    full_rows = gather_mlp(blended_rows, Y_COUNT).astype(jnp.float32)
    row_mean = jnp.sum(full_rows, axis=(0, 2)) / MODEL_WIDTH
    variance = jnp.sum(full_rows * full_rows, axis=(0, 2)) / MODEL_WIDTH - row_mean * row_mean
    inv = lax.rsqrt(variance + norm_epsilon)
    scale_m = (1.0 + scale_rows).reshape(-1, mlp_count, width).transpose(1, 0, 2)
    shift_m = shift_rows.reshape(-1, mlp_count, width).transpose(1, 0, 2)
    normalized = (
        (full_rows - row_mean[None, :, None]) * inv[None, :, None] * scale_m + shift_m
    ).astype(jnp.bfloat16)

    normed_local = lax.dynamic_index_in_dim(normalized, column_index, 0, keepdims=False)
    part_low = jnp.dot(
        normed_local,
        hidden_down_maps.reshape(width, ADAPTER_TOTAL * ADAPTER_RANK),
        preferred_element_type=jnp.float32,
    )
    hidden_rank_values = mlp_sum(select_low(part_low, adapter_hot).astype(jnp.bfloat16)).astype(
        jnp.bfloat16
    )
    hidden_units = up_weight.shape[1]
    hidden_total = jnp.einsum(
        "mtc,mch->th",
        normalized,
        up_w.reshape(mlp_count, width, hidden_units),
        preferred_element_type=jnp.float32,
    )
    hidden_total = hidden_total + jnp.dot(
        expand_rank_rows(hidden_rank_values, adapter_hot),
        hidden_up_maps.reshape(ADAPTER_TOTAL * ADAPTER_RANK, hidden_units),
        preferred_element_type=jnp.float32,
    )
    hidden = jax.nn.gelu(hidden_total, approximate=True).astype(jnp.bfloat16)
    core = column_index % 2
    down_by_core = down_t.reshape(Y_COUNT, mlp_count // Y_COUNT, width, hidden_units)
    half_rows = tok_dev // 2
    halves = []
    for start in (0, half_rows):
        rows = hidden[start : start + half_rows]
        down_parts = [
            jnp.einsum(
                "th,ych->ytc",
                rows,
                lax.dynamic_index_in_dim(down_by_core, pick, 1, keepdims=False),
                preferred_element_type=jnp.float32,
            ).astype(jnp.bfloat16)
            for pick in (1 - core, core)
        ]
        halves.append(scatter_pair(lax.optimization_barrier(down_parts[1]), down_parts[0]))
    down_sum = jnp.concatenate(halves, axis=0)
    result = (values + gate_rows * down_sum).astype(jnp.bfloat16)
    return result.reshape(tok_dev, 1, width)


def solution(mesh):
    placed = (
        P("req", "mlp"),
        P("req", "mlp"),
        P(),
        P(),
        P(),
        P("mlp", "req"),
        P("mlp", None, None),
        P(None, None, "mlp"),
        P(),
        P("mlp", None, None),
        P(None, None, "mlp"),
        P("req", "mlp"),
        P("mlp", "req"),
    )
    return jax.shard_map(
        local, mesh=mesh, in_specs=placed, out_specs=P(None, "req", "mlp"), check_vma=False
    )
```
